32 devices in a mesh: blk: 8 (over z, x), cent: 4 (over y, core).
Axes of the slice: x: 2, y: 2, z: 4, core: 2. Of those that a mesh axis runs over, the one named last changes fastest.
Arguments:
- descriptors: bfloat16 [6144, 1024], P('blk'), may hold values from -6 to 6
- landmarks: bfloat16 [4096, 1024], P('blk'), may hold values from -6 to 6
- whitening: bfloat16 [4096, 4096], P('blk', 'cent'), may hold values from -0.09375 to 0.09375
- centroids: bfloat16 [4096, 4096], P('cent'), may hold values from -8 to 8, as said below
Outputs:
- assign: bfloat16 [6144, 4096], P('blk', 'cent')
- new_centroids: float32 [4096, 4096], P('blk', 'cent')
The draws below stay inside these ranges and needn't reach their ends.
Inputs may be any that keep to these rules, and one draw needn't show every extreme that they name: `centroids`: centroid coordinates.
All inputs are finite; a program needn't handle non-finite values.
Results may differ from the reference program's by a relative error of at most 0.03.
Values may be sent and summed in bfloat16 or wider, within the bound.
No kernel may reach another device: no remote copies, remote signals or barrier semaphores. Data moves between devices by JAX's collectives and lax.ppermute only.
A program may use at most 128 MiB of HBM per device.

```python
import math
import jax
import jax.numpy as jnp
from jax import lax

D = 1024
M = 4096
R = 4096
C = 4096
N = 6144


def draw_centroids(key, part):
    base = jax.random.normal(key, (C, R), jnp.float32) * R ** (-0.5)
    return jnp.clip(base, -8.0, 8.0).astype(jnp.bfloat16)


def block_levels(own_key, extent, shards, low, top_value):
    factor_of, own = 1.0, jax.random.fold_in(own_key, 6)
    for dim, blocks in shards:
        draws = jnp.exp(jax.random.uniform(jax.random.fold_in(own, dim), (blocks,), jnp.float32, low / len(shards), top_value / len(shards)))
        factor_of = factor_of * jnp.repeat(draws, extent[dim] // blocks).reshape([-1 if axis == dim else 1 for axis in range(len(extent))])
    return factor_of


def centred(stream_key, extent, width, reach, split=(), dtype=jnp.bfloat16):
    drawn = width * jax.random.normal(stream_key, extent, jnp.float32)
    if split:
        drawn = drawn * block_levels(stream_key, extent, split, -0.22, 0.18)
    return jnp.clip(drawn, -reach, reach).astype(dtype)


def setup_inputs(seed: int = 0) -> dict:
    arg_keys = jax.random.split(jax.random.key(seed), 5)
    return {
        "descriptors": centred(arg_keys[0], (N, D), 1.0, 6.0, ((0, 8),)),
        "landmarks": centred(arg_keys[1], (M, D), 1.0, 6.0, ((0, 8),)),
        "whitening": centred(arg_keys[2], (M, R), M ** -0.5, 0.09375, ((0, 8), (1, 4))),
        "centroids": draw_centroids(jax.random.fold_in(arg_keys[4], 71), 0),
    }


def unit_rows(values):
    wide = values.astype(jnp.float32)
    sum_sq = lax.optimization_barrier(jnp.sum(wide * wide, axis=1, keepdims=True))
    scale = lax.rsqrt(sum_sq + 1e-06)
    return (wide * scale).astype(jnp.bfloat16)

def reference(descriptors, landmarks, whitening, centroids):
    unit_desc = unit_rows(descriptors)
    unit_land = unit_rows(landmarks)
    sharpness = math.sqrt(D)
    cosine = jnp.dot(unit_desc, unit_land.T, preferred_element_type=jnp.float32)
    kernel = jnp.exp(sharpness * cosine).astype(jnp.bfloat16)
    features = jnp.dot(kernel, whitening, preferred_element_type=jnp.float32).astype(jnp.bfloat16)
    logits = jnp.dot(features, centroids.T, preferred_element_type=jnp.float32)
    row_top = lax.optimization_barrier(jnp.max(logits, axis=1, keepdims=True))
    weights = jnp.exp(logits - row_top)
    row_total = lax.optimization_barrier(jnp.sum(weights, axis=1, keepdims=True))
    assign = (weights / row_total).astype(jnp.bfloat16)
    counts = lax.optimization_barrier(jnp.sum(assign.astype(jnp.float32), axis=0))
    sums = jnp.dot(features.T, assign, preferred_element_type=jnp.float32)
    return (assign, sums / jnp.maximum(counts, 1.0)[None, :])
```

```python
import math

import jax
import jax.numpy as jnp
from jax import lax
from jax.sharding import PartitionSpec as P


def unit_rows(values):
    wide = values.astype(jnp.float32)
    sum_sq = jnp.sum(wide * wide, axis=1, keepdims=True)
    scale = lax.rsqrt(sum_sq + 1e-06)
    return (wide * scale).astype(jnp.bfloat16)


def ring_order(nb):
    if nb % 2:
        return list(range(nb))
    half = nb // 2
    return [2 * i for i in range(half)] + [2 * i + 1 for i in reversed(range(half))]


def make_per_device(nb, nc):
    ring = ring_order(nb)
    pos_of = [0] * nb
    for i, b in enumerate(ring):
        pos_of[b] = i
    fwd = [(ring[i], ring[(i + 1) % nb]) for i in range(nb)]
    bwd = [(ring[(i + 1) % nb], ring[i]) for i in range(nb)]
    ring_arr = jnp.array(ring, jnp.int32)
    pos_arr = jnp.array(pos_of, jnp.int32)

    def per_device(descriptors, landmarks, whitening, centroids):
        me = lax.axis_index("blk")
        cme = lax.axis_index("cent")
        p = pos_arr[me]

        def ring_blk(i):
            return ring_arr[i % nb]

        unit_desc = unit_rows(descriptors)
        unit_land = unit_rows(landmarks)
        ml = unit_land.shape[0]
        q = ml // nc
        quarter = lax.dynamic_slice_in_dim(unit_land, cme * q, q, axis=0)
        lq = lax.all_gather(quarter, "blk", axis=0, tiled=False)
        lall = lax.all_gather(lq, "cent", axis=0, tiled=False)
        land_full = jnp.transpose(lall, (1, 0, 2, 3)).reshape(nb * ml, -1)

        sharpness = math.sqrt(descriptors.shape[1])
        cosine = lax.dot_general(
            unit_desc, land_full, (((1,), (1,)), ((), ())), preferred_element_type=jnp.float32
        )
        kernel = jnp.exp(sharpness * cosine).astype(jnp.bfloat16)

        mw = whitening.shape[0]
        h = mw // 2

        def kcols(blk, off):
            return lax.dynamic_slice_in_dim(kernel, blk * mw + off, h, axis=1)

        wa = whitening[:h]
        wb = whitening[h:]
        acc = jnp.dot(kcols(me, 0), wa, preferred_element_type=jnp.float32)
        acc = acc + jnp.dot(kcols(me, h), wb, preferred_element_type=jnp.float32)

        def w_step(s, carry):
            wa, wb, acc = carry
            na = lax.ppermute(wa, "blk", fwd)
            nbk = lax.ppermute(wb, "blk", bwd)
            if s is not None:
                acc = acc + jnp.dot(kcols(ring_blk(p - s), 0), wa, preferred_element_type=jnp.float32)
                acc = acc + jnp.dot(kcols(ring_blk(p + s), h), wb, preferred_element_type=jnp.float32)
            return na, nbk, acc

        wa, wb, _ = w_step(None, (wa, wb, acc))
        wa, wb, acc = lax.fori_loop(1, nb - 1, w_step, (wa, wb, acc))
        s_last = nb - 1
        acc = acc + jnp.dot(kcols(ring_blk(p - s_last), 0), wa, preferred_element_type=jnp.float32)
        acc = acc + jnp.dot(kcols(ring_blk(p + s_last), h), wb, preferred_element_type=jnp.float32)
        feature_cols = acc.astype(jnp.bfloat16)

        features = lax.all_gather(feature_cols, "cent", axis=1, tiled=True)
        logits = lax.dot_general(
            features, centroids, (((1,), (1,)), ((), ())), preferred_element_type=jnp.float32
        )
        local_top = jnp.max(logits, axis=1)
        row_top = lax.pmax(local_top, "cent")
        weights = jnp.exp(logits - row_top[:, None])
        row_total = lax.psum(jnp.sum(weights, axis=1), "cent")
        assign = (weights / row_total[:, None]).astype(jnp.bfloat16)
        part_counts = jnp.sum(assign.astype(jnp.float32), axis=0)
        counts = jnp.sum(lax.all_gather(part_counts, "blk", axis=0, tiled=False), axis=0)

        rb = features.shape[1] // nb
        rh = rb // 2

        def part_sums(blk, off):
            cols = lax.dynamic_slice_in_dim(features, blk * rb + off, rh, axis=1)
            return lax.dot_general(
                cols, assign, (((0,), (0,)), ((), ())), preferred_element_type=jnp.float32
            )

        def r_step(s, carry):
            acc_a, acc_b = carry
            ra = lax.ppermute(acc_a.astype(jnp.bfloat16), "blk", fwd)
            rbk = lax.ppermute(acc_b.astype(jnp.bfloat16), "blk", bwd)
            acc_a = ra.astype(jnp.float32) + part_sums(ring_blk(p - 1 - s), 0)
            acc_b = rbk.astype(jnp.float32) + part_sums(ring_blk(p + 1 + s), rh)
            return acc_a, acc_b

        acc_a = part_sums(ring_blk(p - 1), 0)
        acc_b = part_sums(ring_blk(p + 1), rh)
        acc_a, acc_b = lax.fori_loop(1, nb, r_step, (acc_a, acc_b))
        sums = jnp.concatenate([acc_a, acc_b], axis=0)
        return (assign, sums / jnp.maximum(counts, 1.0)[None, :])

    return per_device


def solution(mesh):
    in_specs = (P("blk", None), P("blk", None), P("blk", "cent"), P("cent", None))
    out_specs = (P("blk", "cent"), P("blk", "cent"))
    per_device = make_per_device(mesh.shape["blk"], mesh.shape["cent"])
    return jax.shard_map(
        per_device, mesh=mesh, in_specs=in_specs, out_specs=out_specs, check_vma=False
    )
```

```python
import math

import jax
import jax.numpy as jnp
from jax import lax
from jax.sharding import PartitionSpec as P


def unit_rows(values):
    wide = values.astype(jnp.float32)
    sum_sq = jnp.sum(wide * wide, axis=1, keepdims=True)
    scale = lax.rsqrt(sum_sq + 1e-06)
    return (wide * scale).astype(jnp.bfloat16)


def ring_order(nb):
    if nb % 2:
        return list(range(nb))
    half = nb // 2
    return [2 * i for i in range(half)] + [2 * i + 1 for i in reversed(range(half))]


def run_steps(first, last, step, carry, unroll):
    if unroll:
        for s in range(first, last):
            carry = step(s, carry)
        return carry
    return lax.fori_loop(first, last, step, carry)


def make_per_device(nb, nc):
    ring = ring_order(nb)
    pos_of = [0] * nb
    for i, b in enumerate(ring):
        pos_of[b] = i
    fwd = [(ring[i], ring[(i + 1) % nb]) for i in range(nb)]
    bwd = [(ring[(i + 1) % nb], ring[i]) for i in range(nb)]
    mates = [(c, c ^ 1) for c in range(nc)]
    ring_arr = jnp.array(ring, jnp.int32)
    pos_arr = jnp.array(pos_of, jnp.int32)
    unroll = nb <= 8

    def per_device(descriptors, landmarks, whitening, centroids):
        me = lax.axis_index("blk")
        cme = lax.axis_index("cent")
        par = cme % 2
        p = pos_arr[me]

        def ring_blk(i):
            return ring_arr[i % nb]

        unit_desc = unit_rows(descriptors)
        unit_land = unit_rows(landmarks)
        sharpness = math.sqrt(descriptors.shape[1])
        mw = whitening.shape[0]
        h = mw // 2
        qh = h // 2

        def feat_part(land_rows, w_rows):
            cos = lax.dot_general(
                unit_desc, land_rows, (((1,), (1,)), ((), ())), preferred_element_type=jnp.float32
            )
            kern = jnp.exp(sharpness * cos).astype(jnp.bfloat16)
            return jnp.dot(kern, w_rows, preferred_element_type=jnp.float32)

        la = lax.dynamic_slice_in_dim(unit_land, par * qh, qh, axis=0)
        lb = lax.dynamic_slice_in_dim(unit_land, h + par * qh, qh, axis=0)
        msg_a = jnp.concatenate([whitening[:h], la], axis=0)
        msg_b = jnp.concatenate([whitening[h:], lb], axis=0)
        acc = feat_part(unit_land, whitening)

        def order(mine, theirs):
            return jnp.where(par == 0, jnp.concatenate([mine, theirs], 0), jnp.concatenate([theirs, mine], 0))

        def w_step(s, carry):
            msg_a, msg_b, acc = carry
            msg_a = lax.ppermute(msg_a, "blk", fwd)
            msg_b = lax.ppermute(msg_b, "blk", bwd)
            theirs = lax.ppermute(jnp.concatenate([msg_a[h:], msg_b[h:]], 0), "cent", mates)
            land_a = order(msg_a[h:], theirs[:qh])
            land_b = order(msg_b[h:], theirs[qh:])
            acc = acc + feat_part(land_a, msg_a[:h]) + feat_part(land_b, msg_b[:h])
            return msg_a, msg_b, acc

        _, _, acc = run_steps(1, nb, w_step, (msg_a, msg_b, acc), unroll)
        feature_cols = acc.astype(jnp.bfloat16)

        features = lax.all_gather(feature_cols, "cent", axis=1, tiled=True)
        logits = lax.dot_general(
            features, centroids, (((1,), (1,)), ((), ())), preferred_element_type=jnp.float32
        )
        local_top = jnp.max(logits, axis=1)
        row_top = lax.pmax(local_top, "cent")
        weights = jnp.exp(logits - row_top[:, None])
        row_total = lax.psum(jnp.sum(weights, axis=1), "cent")
        assign = (weights / row_total[:, None]).astype(jnp.bfloat16)
        part_counts = jnp.sum(assign.astype(jnp.float32), axis=0)

        rb = features.shape[1] // nb
        rh = rb // 2

        def part_sums(blk, off):
            cols = lax.dynamic_slice_in_dim(features, blk * rb + off, rh, axis=1)
            return lax.optimization_barrier(
                lax.dot_general(
                    cols, assign, (((0,), (0,)), ((), ())), preferred_element_type=jnp.float32
                )
            )

        def r_step(s, carry):
            acc_a, acc_b, cnt_send, cnt = carry
            ra = lax.ppermute(acc_a.astype(jnp.bfloat16), "blk", fwd)
            rbk = lax.ppermute(acc_b.astype(jnp.bfloat16), "blk", bwd)
            cnt_send = lax.ppermute(cnt_send, "blk", fwd)
            pa = part_sums(ring_blk(p - 1 - s), 0)
            pb = part_sums(ring_blk(p + 1 + s), rh)
            return ra.astype(jnp.float32) + pa, rbk.astype(jnp.float32) + pb, cnt_send, cnt + cnt_send

        acc_a = part_sums(ring_blk(p - 1), 0)
        acc_b = part_sums(ring_blk(p + 1), rh)
        acc_a, acc_b, _, counts = run_steps(
            1, nb, r_step, (acc_a, acc_b, part_counts, part_counts), unroll
        )
        sums = jnp.concatenate([acc_a, acc_b], axis=0)
        return (assign, sums / jnp.maximum(counts, 1.0)[None, :])

    return per_device


def solution(mesh):
    in_specs = (P("blk", None), P("blk", None), P("blk", "cent"), P("cent", None))
    out_specs = (P("blk", "cent"), P("blk", "cent"))
    per_device = make_per_device(mesh.shape["blk"], mesh.shape["cent"])
    return jax.shard_map(
        per_device, mesh=mesh, in_specs=in_specs, out_specs=out_specs, check_vma=False
    )
```

```python
import math

import jax
import jax.numpy as jnp
from jax import lax
from jax.sharding import PartitionSpec as P


def unit_rows(values):
    wide = values.astype(jnp.float32)
    sum_sq = jnp.sum(wide * wide, axis=1, keepdims=True)
    scale = lax.rsqrt(sum_sq + 1e-06)
    return (wide * scale).astype(jnp.bfloat16)


def ring_order(nb):
    if nb % 2:
        return list(range(nb))
    half = nb // 2
    return [2 * i for i in range(half)] + [2 * i + 1 for i in reversed(range(half))]


def run_steps(first, last, step, carry, unroll):
    if unroll:
        for s in range(first, last):
            carry = step(s, carry)
        return carry
    return lax.fori_loop(first, last, step, carry)


def make_per_device(nb, nc):
    ring = ring_order(nb)
    pos_of = [0] * nb
    for i, b in enumerate(ring):
        pos_of[b] = i
    fwd = [(ring[i], ring[(i + 1) % nb]) for i in range(nb)]
    bwd = [(ring[(i + 1) % nb], ring[i]) for i in range(nb)]
    mates = [(c, c ^ 1) for c in range(nc)]
    ring_arr = jnp.array(ring, jnp.int32)
    pos_arr = jnp.array(pos_of, jnp.int32)
    unroll = nb <= 8

    def per_device(descriptors, landmarks, whitening, centroids):
        me = lax.axis_index("blk")
        cme = lax.axis_index("cent")
        par = cme % 2
        p = pos_arr[me]

        def ring_blk(i):
            return ring_arr[i % nb]

        unit_desc = unit_rows(descriptors)
        unit_land = unit_rows(landmarks)
        sharpness = math.sqrt(descriptors.shape[1])
        mw = whitening.shape[0]
        h = mw // 2
        qh = h // 2

        def feat_part(land_rows, w_rows):
            cos = lax.dot_general(
                unit_desc, land_rows, (((1,), (1,)), ((), ())), preferred_element_type=jnp.float32
            )
            kern = jnp.exp(sharpness * cos).astype(jnp.bfloat16)
            return jnp.dot(kern, w_rows, preferred_element_type=jnp.float32)

        la = lax.dynamic_slice_in_dim(unit_land, par * qh, qh, axis=0)
        lb = lax.dynamic_slice_in_dim(unit_land, h + par * qh, qh, axis=0)
        msg_a = jnp.concatenate([whitening[:h], la], axis=0)
        msg_b = jnp.concatenate([whitening[h:], lb], axis=0)
        acc = feat_part(unit_land, whitening)

        def order(mine, theirs):
            return jnp.where(par == 0, jnp.concatenate([mine, theirs], 0), jnp.concatenate([theirs, mine], 0))

        def w_step(s, carry):
            msg_a, msg_b, acc = carry
            msg_a = lax.ppermute(msg_a, "blk", fwd)
            msg_b = lax.ppermute(msg_b, "blk", bwd)
            theirs = lax.ppermute(jnp.concatenate([msg_a[h:], msg_b[h:]], 0), "cent", mates)
            land = jnp.concatenate(
                [order(msg_a[h:], theirs[:qh]), order(msg_b[h:], theirs[qh:])], 0
            )
            wrows = jnp.concatenate([msg_a[:h], msg_b[:h]], 0)
            acc = lax.optimization_barrier(acc + feat_part(land, wrows))
            return msg_a, msg_b, acc
        _, _, acc = run_steps(1, nb, w_step, (msg_a, msg_b, acc), unroll)
        feature_cols = acc.astype(jnp.bfloat16)

        features = lax.all_gather(feature_cols, "cent", axis=1, tiled=True)
        logits = lax.dot_general(
            features, centroids, (((1,), (1,)), ((), ())), preferred_element_type=jnp.float32
        )
        local_top = jnp.max(logits, axis=1)
        local_sum = jnp.sum(jnp.exp(logits - local_top[:, None]), axis=1)
        stats = jnp.stack([local_top, local_sum], 0)
        peers = [stats] + [
            lax.ppermute(stats, "cent", [(c, (c + k) % nc) for c in range(nc)]) for k in range(1, nc)
        ]
        row_top = peers[0][0]
        for st in peers[1:]:
            row_top = jnp.maximum(row_top, st[0])
        row_total = peers[0][1] * jnp.exp(peers[0][0] - row_top)
        for st in peers[1:]:
            row_total = row_total + st[1] * jnp.exp(st[0] - row_top)
        weights = jnp.exp(logits - row_top[:, None])
        assign = (weights / row_total[:, None]).astype(jnp.bfloat16)
        part_counts = jnp.sum(assign.astype(jnp.float32), axis=0)

        rb = features.shape[1] // nb
        rh = rb // 2

        def part_sums(blk, off):
            cols = lax.dynamic_slice_in_dim(features, blk * rb + off, rh, axis=1)
            return lax.optimization_barrier(
                lax.dot_general(
                    cols, assign, (((0,), (0,)), ((), ())), preferred_element_type=jnp.float32
                )
            )

        def r_step(s, carry):
            acc_a, acc_b, cnt_send, cnt = carry
            ra = lax.ppermute(acc_a.astype(jnp.bfloat16), "blk", fwd)
            rbk = lax.ppermute(acc_b.astype(jnp.bfloat16), "blk", bwd)
            cnt_send = lax.ppermute(cnt_send, "blk", fwd)
            pa = part_sums(ring_blk(p - 1 - s), 0)
            pb = part_sums(ring_blk(p + 1 + s), rh)
            return ra.astype(jnp.float32) + pa, rbk.astype(jnp.float32) + pb, cnt_send, cnt + cnt_send

        acc_a = part_sums(ring_blk(p - 1), 0)
        acc_b = part_sums(ring_blk(p + 1), rh)
        acc_a, acc_b, _, counts = run_steps(
            1, nb, r_step, (acc_a, acc_b, part_counts, part_counts), unroll
        )
        sums = jnp.concatenate([acc_a, acc_b], axis=0)
        return (assign, sums / jnp.maximum(counts, 1.0)[None, :])

    return per_device


def solution(mesh):
    in_specs = (P("blk", None), P("blk", None), P("blk", "cent"), P("cent", None))
    out_specs = (P("blk", "cent"), P("blk", "cent"))
    per_device = make_per_device(mesh.shape["blk"], mesh.shape["cent"])
    return jax.shard_map(
        per_device, mesh=mesh, in_specs=in_specs, out_specs=out_specs, check_vma=False
    )
```

```python
import math

import jax
import jax.numpy as jnp
from jax import lax
from jax.sharding import PartitionSpec as P


def unit_rows(values):
    wide = values.astype(jnp.float32)
    sum_sq = jnp.sum(wide * wide, axis=1, keepdims=True)
    scale = lax.rsqrt(sum_sq + 1e-06)
    return (wide * scale).astype(jnp.bfloat16)


def ring_order(nb):
    if nb % 2:
        return list(range(nb))
    half = nb // 2
    return [2 * i for i in range(half)] + [2 * i + 1 for i in reversed(range(half))]


def run_steps(first, last, step, carry, unroll):
    if unroll:
        for s in range(first, last):
            carry = step(s, carry)
        return carry
    return lax.fori_loop(first, last, step, carry)


def make_per_device(nb, nc):
    ring = ring_order(nb)
    pos_of = [0] * nb
    for i, b in enumerate(ring):
        pos_of[b] = i
    fwd = [(ring[i], ring[(i + 1) % nb]) for i in range(nb)]
    bwd = [(ring[(i + 1) % nb], ring[i]) for i in range(nb)]
    mates = [(c, c ^ 1) for c in range(nc)]
    ring_arr = jnp.array(ring, jnp.int32)
    pos_arr = jnp.array(pos_of, jnp.int32)
    unroll = nb <= 8

    def per_device(descriptors, landmarks, whitening, centroids):
        me = lax.axis_index("blk")
        cme = lax.axis_index("cent")
        par = cme % 2
        p = pos_arr[me]

        def ring_blk(i):
            return ring_arr[i % nb]

        unit_desc = unit_rows(descriptors)
        unit_land = unit_rows(landmarks)
        sharpness = math.sqrt(descriptors.shape[1])
        mw = whitening.shape[0]
        h = mw // 2
        qh = h // 2

        def feat_part(land_rows, w_rows):
            cos = lax.dot_general(
                unit_desc, land_rows, (((1,), (1,)), ((), ())), preferred_element_type=jnp.float32
            )
            kern = jnp.exp(sharpness * cos).astype(jnp.bfloat16)
            return jnp.dot(kern, w_rows, preferred_element_type=jnp.float32)

        la = lax.dynamic_slice_in_dim(unit_land, par * qh, qh, axis=0)
        lb = lax.dynamic_slice_in_dim(unit_land, h + par * qh, qh, axis=0)
        acc = feat_part(unit_land, whitening)

        def order(mine, theirs):
            return jnp.where(par == 0, jnp.concatenate([mine, theirs], 0), jnp.concatenate([theirs, mine], 0))

        def w_step(s, carry):
            wa, wb, la, lb, acc = carry
            wa = lax.ppermute(wa, "blk", fwd)
            wb = lax.ppermute(wb, "blk", bwd)
            la = lax.ppermute(la, "blk", fwd)
            lb = lax.ppermute(lb, "blk", bwd)
            ta = lax.ppermute(la, "cent", mates)
            tb = lax.ppermute(lb, "cent", mates)
            land = jnp.concatenate([order(la, ta), order(lb, tb)], 0)
            wrows = jnp.concatenate([wa, wb], 0)
            acc = lax.optimization_barrier(acc + feat_part(land, wrows))
            return wa, wb, la, lb, acc

        carry = (whitening[:h], whitening[h:], la, lb, acc)
        *_, acc = run_steps(1, nb, w_step, carry, unroll)
        feature_cols = acc.astype(jnp.bfloat16)

        features = lax.all_gather(feature_cols, "cent", axis=1, tiled=True)
        logits = lax.dot_general(
            features, centroids, (((1,), (1,)), ((), ())), preferred_element_type=jnp.float32
        )
        local_top = jnp.max(logits, axis=1)
        local_sum = jnp.sum(jnp.exp(logits - local_top[:, None]), axis=1)
        stats = jnp.stack([local_top, local_sum], 0)
        peers = [stats] + [
            lax.ppermute(stats, "cent", [(c, (c + k) % nc) for c in range(nc)]) for k in range(1, nc)
        ]
        row_top = peers[0][0]
        for st in peers[1:]:
            row_top = jnp.maximum(row_top, st[0])
        row_total = peers[0][1] * jnp.exp(peers[0][0] - row_top)
        for st in peers[1:]:
            row_total = row_total + st[1] * jnp.exp(st[0] - row_top)
        weights = jnp.exp(logits - row_top[:, None])
        assign = (weights / row_total[:, None]).astype(jnp.bfloat16)
        part_counts = jnp.sum(assign.astype(jnp.float32), axis=0)

        rb = features.shape[1] // nb
        rh = rb // 2

        def part_sums(blk, off):
            cols = lax.dynamic_slice_in_dim(features, blk * rb + off, rh, axis=1)
            return lax.optimization_barrier(
                lax.dot_general(
                    cols, assign, (((0,), (0,)), ((), ())), preferred_element_type=jnp.float32
                )
            )

        def r_step(s, carry):
            acc_a, acc_b, cnt_send, cnt = carry
            ra = lax.ppermute(acc_a.astype(jnp.bfloat16), "blk", fwd)
            rbk = lax.ppermute(acc_b.astype(jnp.bfloat16), "blk", bwd)
            cnt_send = lax.ppermute(cnt_send, "blk", fwd)
            pa = part_sums(ring_blk(p - 1 - s), 0)
            pb = part_sums(ring_blk(p + 1 + s), rh)
            return ra.astype(jnp.float32) + pa, rbk.astype(jnp.float32) + pb, cnt_send, cnt + cnt_send

        acc_a = part_sums(ring_blk(p - 1), 0)
        acc_b = part_sums(ring_blk(p + 1), rh)
        acc_a, acc_b, _, counts = run_steps(
            1, nb, r_step, (acc_a, acc_b, part_counts, part_counts), unroll
        )
        sums = jnp.concatenate([acc_a, acc_b], axis=0)
        return (assign, sums / jnp.maximum(counts, 1.0)[None, :])

    return per_device


def solution(mesh):
    in_specs = (P("blk", None), P("blk", None), P("blk", "cent"), P("cent", None))
    out_specs = (P("blk", "cent"), P("blk", "cent"))
    per_device = make_per_device(mesh.shape["blk"], mesh.shape["cent"])
    return jax.shard_map(
        per_device, mesh=mesh, in_specs=in_specs, out_specs=out_specs, check_vma=False
    )
```

```python
import math

import jax
import jax.numpy as jnp
from jax import lax
from jax.sharding import PartitionSpec as P


def unit_rows(values):
    wide = values.astype(jnp.float32)
    sum_sq = jnp.sum(wide * wide, axis=1, keepdims=True)
    scale = lax.rsqrt(sum_sq + 1e-06)
    return (wide * scale).astype(jnp.bfloat16)


def ring_order(nb):
    if nb % 2:
        return list(range(nb))
    half = nb // 2
    return [2 * i for i in range(half)] + [2 * i + 1 for i in reversed(range(half))]


def run_steps(first, last, step, carry, unroll):
    if unroll:
        for s in range(first, last):
            carry = step(s, carry)
        return carry
    return lax.fori_loop(first, last, step, carry)


def make_per_device(nb, nc):
    ring = ring_order(nb)
    pos_of = [0] * nb
    for i, b in enumerate(ring):
        pos_of[b] = i
    fwd = [(ring[i], ring[(i + 1) % nb]) for i in range(nb)]
    bwd = [(ring[(i + 1) % nb], ring[i]) for i in range(nb)]
    mates = [(c, c ^ 1) for c in range(nc)]
    ring_arr = jnp.array(ring, jnp.int32)
    pos_arr = jnp.array(pos_of, jnp.int32)
    unroll = nb <= 8

    def per_device(descriptors, landmarks, whitening, centroids):
        me = lax.axis_index("blk")
        cme = lax.axis_index("cent")
        par = cme % 2
        p = pos_arr[me]

        def ring_blk(i):
            return ring_arr[i % nb]

        unit_desc = unit_rows(descriptors)
        unit_land = unit_rows(landmarks)
        sharpness = math.sqrt(descriptors.shape[1])
        mw = whitening.shape[0]
        h = mw // 2
        qh = h // 2

        def feat_part(land_rows, w_rows):
            cos = lax.dot_general(
                unit_desc, land_rows, (((1,), (1,)), ((), ())), preferred_element_type=jnp.float32
            )
            kern = jnp.exp(sharpness * cos).astype(jnp.bfloat16)
            return jnp.dot(kern, w_rows, preferred_element_type=jnp.float32)

        la = lax.dynamic_slice_in_dim(unit_land, par * qh, qh, axis=0)
        lb = lax.dynamic_slice_in_dim(unit_land, h + par * qh, qh, axis=0)
        acc = feat_part(unit_land, whitening)

        def mine_first(rows):
            swapped = jnp.concatenate([rows[qh:], rows[:qh]], 0)
            return jnp.where(par == 0, rows, swapped)

        def w_step(s, carry):
            wa, wb, la, lb, acc = carry
            wa = lax.ppermute(wa, "blk", fwd)
            wb = lax.ppermute(wb, "blk", bwd)
            la = lax.ppermute(la, "blk", fwd)
            lb = lax.ppermute(lb, "blk", bwd)
            ta = lax.ppermute(la, "cent", mates)
            tb = lax.ppermute(lb, "cent", mates)
            land = jnp.concatenate([la, ta, lb, tb], 0)
            wrows = jnp.concatenate([wa, wb], 0)
            acc = lax.optimization_barrier(acc + feat_part(land, wrows))
            return wa, wb, la, lb, acc

        carry = (mine_first(whitening[:h]), mine_first(whitening[h:]), la, lb, acc)
        *_, acc = run_steps(1, nb, w_step, carry, unroll)
        feature_cols = acc.astype(jnp.bfloat16)

        cw = feature_cols.shape[1]
        if nc == 4:
            ypair = [(c, c ^ 2) for c in range(nc)]
            from_y = lax.ppermute(feature_cols, "cent", ypair)
            from_mate = lax.ppermute(feature_cols, "cent", mates)
            from_far = lax.ppermute(from_y, "cent", mates)
            pieces = [feature_cols, from_mate, from_y, from_far]
            blocks = [cme ^ t for t in range(nc)]
        else:
            pieces = [feature_cols] + [
                lax.ppermute(feature_cols, "cent", [(c, (c + t) % nc) for c in range(nc)])
                for t in range(1, nc)
            ]
            blocks = [(cme - t) % nc for t in range(nc)]
        logits = None
        for piece, blk in zip(pieces, blocks):
            cpart = lax.dynamic_slice_in_dim(centroids, blk * cw, cw, axis=1)
            part = lax.dot_general(
                piece, cpart, (((1,), (1,)), ((), ())), preferred_element_type=jnp.float32
            )
            logits = part if logits is None else logits + part
        features = jnp.concatenate(pieces, axis=1)
        local_top = jnp.max(logits, axis=1)
        local_sum = jnp.sum(jnp.exp(logits - local_top[:, None]), axis=1)
        stats = jnp.stack([local_top, local_sum], 0)
        peers = [stats] + [
            lax.ppermute(stats, "cent", [(c, (c + k) % nc) for c in range(nc)]) for k in range(1, nc)
        ]
        row_top = peers[0][0]
        for st in peers[1:]:
            row_top = jnp.maximum(row_top, st[0])
        row_total = peers[0][1] * jnp.exp(peers[0][0] - row_top)
        for st in peers[1:]:
            row_total = row_total + st[1] * jnp.exp(st[0] - row_top)
        weights = jnp.exp(logits - row_top[:, None])
        assign = (weights / row_total[:, None]).astype(jnp.bfloat16)
        part_counts = jnp.sum(assign.astype(jnp.float32), axis=0)

        rb = features.shape[1] // nb
        rh = rb // 2

        def part_sums(blk, off):
            col = blk * rb + off
            cblk = col // cw
            if nc == 4:
                t = cblk ^ cme
            else:
                t = (cme - cblk) % nc
            cols = lax.dynamic_slice_in_dim(features, t * cw + col % cw, rh, axis=1)
            return lax.optimization_barrier(
                lax.dot_general(
                    cols, assign, (((0,), (0,)), ((), ())), preferred_element_type=jnp.float32
                )
            )

        def r_step(s, carry):
            acc_a, acc_b, cnt_send, cnt = carry
            ra = lax.ppermute(acc_a.astype(jnp.bfloat16), "blk", fwd)
            rbk = lax.ppermute(acc_b.astype(jnp.bfloat16), "blk", bwd)
            cnt_send = lax.ppermute(cnt_send, "blk", fwd)
            pa = part_sums(ring_blk(p - 1 - s), 0)
            pb = part_sums(ring_blk(p + 1 + s), rh)
            return ra.astype(jnp.float32) + pa, rbk.astype(jnp.float32) + pb, cnt_send, cnt + cnt_send

        acc_a = part_sums(ring_blk(p - 1), 0)
        acc_b = part_sums(ring_blk(p + 1), rh)
        acc_a, acc_b, _, counts = run_steps(
            1, nb, r_step, (acc_a, acc_b, part_counts, part_counts), unroll
        )
        sums = jnp.concatenate([acc_a, acc_b], axis=0)
        return (assign, sums / jnp.maximum(counts, 1.0)[None, :])

    return per_device


def solution(mesh):
    in_specs = (P("blk", None), P("blk", None), P("blk", "cent"), P("cent", None))
    out_specs = (P("blk", "cent"), P("blk", "cent"))
    per_device = make_per_device(mesh.shape["blk"], mesh.shape["cent"])
    return jax.shard_map(
        per_device, mesh=mesh, in_specs=in_specs, out_specs=out_specs, check_vma=False
    )
```

```python
import math

import jax
import jax.numpy as jnp
from jax import lax
from jax.sharding import PartitionSpec as P


def unit_rows(values):
    wide = values.astype(jnp.float32)
    sum_sq = jnp.sum(wide * wide, axis=1, keepdims=True)
    scale = lax.rsqrt(sum_sq + 1e-06)
    return (wide * scale).astype(jnp.bfloat16)


def ring_order(nb):
    if nb % 2:
        return list(range(nb))
    half = nb // 2
    return [2 * i for i in range(half)] + [2 * i + 1 for i in reversed(range(half))]


def run_steps(first, last, step, carry, unroll):
    if unroll:
        for s in range(first, last):
            carry = step(s, carry)
        return carry
    return lax.fori_loop(first, last, step, carry)


def make_per_device(nb, nc):
    ring = ring_order(nb)
    pos_of = [0] * nb
    for i, b in enumerate(ring):
        pos_of[b] = i
    fwd = [(ring[i], ring[(i + 1) % nb]) for i in range(nb)]
    bwd = [(ring[(i + 1) % nb], ring[i]) for i in range(nb)]
    mates = [(c, c ^ 1) for c in range(nc)]
    ring_arr = jnp.array(ring, jnp.int32)
    pos_arr = jnp.array(pos_of, jnp.int32)
    unroll = nb <= 8

    def per_device(descriptors, landmarks, whitening, centroids):
        me = lax.axis_index("blk")
        cme = lax.axis_index("cent")
        par = cme % 2
        p = pos_arr[me]

        def ring_blk(i):
            return ring_arr[i % nb]

        unit_desc = unit_rows(descriptors)
        unit_land = unit_rows(landmarks)
        sharpness = math.sqrt(descriptors.shape[1])
        mw = whitening.shape[0]
        h = mw // 2
        qh = h // 2

        def feat_part(land_rows, w_rows):
            cos = lax.dot_general(
                unit_desc, land_rows, (((1,), (1,)), ((), ())), preferred_element_type=jnp.float32
            )
            kern = jnp.exp(sharpness * cos).astype(jnp.bfloat16)
            return jnp.dot(kern, w_rows, preferred_element_type=jnp.float32)

        la = lax.dynamic_slice_in_dim(unit_land, par * qh, qh, axis=0)
        lb = lax.dynamic_slice_in_dim(unit_land, h + par * qh, qh, axis=0)
        acc = feat_part(unit_land, whitening)

        def mine_first(rows):
            swapped = jnp.concatenate([rows[qh:], rows[:qh]], 0)
            return jnp.where(par == 0, rows, swapped)

        def w_step(s, carry):
            wa, wb, la, lb, acc = carry
            wa = lax.ppermute(wa, "blk", fwd)
            wb = lax.ppermute(wb, "blk", bwd)
            la = lax.ppermute(la, "blk", fwd)
            lb = lax.ppermute(lb, "blk", bwd)
            ta = lax.ppermute(la, "cent", mates)
            tb = lax.ppermute(lb, "cent", mates)
            land = jnp.concatenate([la, ta, lb, tb], 0)
            wrows = jnp.concatenate([wa, wb], 0)
            acc = lax.optimization_barrier(acc + feat_part(land, wrows))
            return wa, wb, la, lb, acc

        carry = (mine_first(whitening[:h]), mine_first(whitening[h:]), la, lb, acc)
        *_, acc = run_steps(1, nb, w_step, carry, unroll)
        feature_cols = acc.astype(jnp.bfloat16)

        cw = feature_cols.shape[1]
        features = lax.all_gather(feature_cols, "cent", axis=1, tiled=True)
        logits = lax.dot_general(
            features, centroids, (((1,), (1,)), ((), ())), preferred_element_type=jnp.float32
        )
        local_top = jnp.max(logits, axis=1)
        local_sum = jnp.sum(jnp.exp(logits - local_top[:, None]), axis=1)
        stats = jnp.stack([local_top, local_sum], 0)
        peers = [stats] + [
            lax.ppermute(stats, "cent", [(c, (c + k) % nc) for c in range(nc)]) for k in range(1, nc)
        ]
        row_top = peers[0][0]
        for st in peers[1:]:
            row_top = jnp.maximum(row_top, st[0])
        row_total = peers[0][1] * jnp.exp(peers[0][0] - row_top)
        for st in peers[1:]:
            row_total = row_total + st[1] * jnp.exp(st[0] - row_top)
        weights = jnp.exp(logits - row_top[:, None])
        assign = (weights / row_total[:, None]).astype(jnp.bfloat16)
        part_counts = jnp.sum(assign.astype(jnp.float32), axis=0)

        rb = features.shape[1] // nb
        rh = rb // 2

        def part_sums(blk, off):
            col = blk * rb + off
            cols = lax.dynamic_slice_in_dim(features, col, rh, axis=1)
            return lax.optimization_barrier(
                lax.dot_general(
                    cols, assign, (((0,), (0,)), ((), ())), preferred_element_type=jnp.float32
                )
            )

        def r_step(s, carry):
            acc_a, acc_b, cnt_send, cnt = carry
            ra = lax.ppermute(acc_a.astype(jnp.bfloat16), "blk", fwd)
            rbk = lax.ppermute(acc_b.astype(jnp.bfloat16), "blk", bwd)
            cnt_send = lax.ppermute(cnt_send, "blk", fwd)
            pa = part_sums(ring_blk(p - 1 - s), 0)
            pb = part_sums(ring_blk(p + 1 + s), rh)
            return ra.astype(jnp.float32) + pa, rbk.astype(jnp.float32) + pb, cnt_send, cnt + cnt_send

        acc_a = part_sums(ring_blk(p - 1), 0)
        acc_b = part_sums(ring_blk(p + 1), rh)
        acc_a, acc_b, _, counts = run_steps(
            1, nb, r_step, (acc_a, acc_b, part_counts, part_counts), unroll
        )
        sums = jnp.concatenate([acc_a, acc_b], axis=0)
        return (assign, sums / jnp.maximum(counts, 1.0)[None, :])

    return per_device


def solution(mesh):
    in_specs = (P("blk", None), P("blk", None), P("blk", "cent"), P("cent", None))
    out_specs = (P("blk", "cent"), P("blk", "cent"))
    per_device = make_per_device(mesh.shape["blk"], mesh.shape["cent"])
    return jax.shard_map(
        per_device, mesh=mesh, in_specs=in_specs, out_specs=out_specs, check_vma=False
    )
```

```python
import math

import jax
import jax.numpy as jnp
from jax import lax
from jax.sharding import PartitionSpec as P


def unit_rows(values):
    wide = values.astype(jnp.float32)
    sum_sq = jnp.sum(wide * wide, axis=1, keepdims=True)
    scale = lax.rsqrt(sum_sq + 1e-06)
    return (wide * scale).astype(jnp.bfloat16)


def ring_order(nb):
    if nb % 2:
        return list(range(nb))
    half = nb // 2
    return [2 * i for i in range(half)] + [2 * i + 1 for i in reversed(range(half))]


def run_steps(first, last, step, carry, unroll):
    if unroll:
        for s in range(first, last):
            carry = step(s, carry)
        return carry
    return lax.fori_loop(first, last, step, carry)


def make_per_device(nb, nc):
    ring = ring_order(nb)
    pos_of = [0] * nb
    for i, b in enumerate(ring):
        pos_of[b] = i
    fwd = [(ring[i], ring[(i + 1) % nb]) for i in range(nb)]
    bwd = [(ring[(i + 1) % nb], ring[i]) for i in range(nb)]
    mates = [(c, c ^ 1) for c in range(nc)]
    snake = nb % 2 == 0
    half_nb = nb // 2

    def pos_of_blk(b):
        if not snake:
            return b
        return jnp.where(b % 2 == 0, b // 2, nb - 1 - b // 2)

    def blk_at(i):
        i = i % nb
        if not snake:
            return i
        return jnp.where(i < half_nb, 2 * i, 2 * (nb - 1 - i) + 1)
    unroll = nb <= 8

    def per_device(descriptors, landmarks, whitening, centroids):
        me = lax.axis_index("blk")
        cme = lax.axis_index("cent")
        par = cme % 2
        p = pos_of_blk(me)

        def ring_blk(i):
            return blk_at(i)

        unit_desc = unit_rows(descriptors)
        unit_land = unit_rows(landmarks)
        sharpness = math.sqrt(descriptors.shape[1])
        mw = whitening.shape[0]
        h = mw // 2
        qh = h // 2

        def feat_part(land_rows, w_rows):
            cos = lax.dot_general(
                unit_desc, land_rows, (((1,), (1,)), ((), ())), preferred_element_type=jnp.float32
            )
            kern = jnp.exp(sharpness * cos).astype(jnp.bfloat16)
            return jnp.dot(kern, w_rows, preferred_element_type=jnp.float32)

        la = lax.dynamic_slice_in_dim(unit_land, par * qh, qh, axis=0)
        lb = lax.dynamic_slice_in_dim(unit_land, h + par * qh, qh, axis=0)
        acc = feat_part(unit_land, whitening)

        def mine_first(rows):
            swapped = jnp.concatenate([rows[qh:], rows[:qh]], 0)
            return jnp.where(par == 0, rows, swapped)

        def w_step(s, carry):
            wa, wb, la, lb, acc = carry
            wa = lax.ppermute(wa, "blk", fwd)
            wb = lax.ppermute(wb, "blk", bwd)
            la = lax.ppermute(la, "blk", fwd)
            lb = lax.ppermute(lb, "blk", bwd)
            ta = lax.ppermute(la, "cent", mates)
            tb = lax.ppermute(lb, "cent", mates)
            land = jnp.concatenate([la, ta, lb, tb], 0)
            wrows = jnp.concatenate([wa, wb], 0)
            acc = lax.optimization_barrier(acc + feat_part(land, wrows))
            return wa, wb, la, lb, acc

        carry = (mine_first(whitening[:h]), mine_first(whitening[h:]), la, lb, acc)
        *_, acc = run_steps(1, nb, w_step, carry, unroll)
        feature_cols = acc.astype(jnp.bfloat16)

        cw = feature_cols.shape[1]
        if nc == 4:
            ypair = [(c, c ^ 2) for c in range(nc)]
            nrow = feature_cols.shape[0]
            nchunk = 4 if nrow % 64 == 0 else 1
            step = nrow // nchunk
            ys, fars = [], []
            for j in range(nchunk):
                y_j = lax.ppermute(feature_cols[j * step:(j + 1) * step], "cent", ypair)
                ys.append(y_j)
                fars.append(lax.ppermute(y_j, "cent", mates))
            from_mate = lax.ppermute(feature_cols, "cent", mates)
            pieces = [feature_cols, from_mate, jnp.concatenate(ys, 0), jnp.concatenate(fars, 0)]
            blocks = [cme ^ t for t in range(nc)]
        else:
            pieces = [feature_cols] + [
                lax.ppermute(feature_cols, "cent", [(c, (c + t) % nc) for c in range(nc)])
                for t in range(1, nc)
            ]
            blocks = [(cme - t) % nc for t in range(nc)]
        logits = None
        for piece, blk in zip(pieces, blocks):
            cpart = lax.dynamic_slice_in_dim(centroids, blk * cw, cw, axis=1)
            part = lax.dot_general(
                piece, cpart, (((1,), (1,)), ((), ())), preferred_element_type=jnp.float32
            )
            logits = part if logits is None else logits + part
        features = jnp.concatenate(pieces, axis=1)
        local_top = jnp.max(logits, axis=1)
        local_sum = jnp.sum(jnp.exp(logits - local_top[:, None]), axis=1)
        stats = jnp.stack([local_top, local_sum], 0)
        peers = [stats] + [
            lax.ppermute(stats, "cent", [(c, (c + k) % nc) for c in range(nc)]) for k in range(1, nc)
        ]
        row_top = peers[0][0]
        for st in peers[1:]:
            row_top = jnp.maximum(row_top, st[0])
        row_total = peers[0][1] * jnp.exp(peers[0][0] - row_top)
        for st in peers[1:]:
            row_total = row_total + st[1] * jnp.exp(st[0] - row_top)
        weights = jnp.exp(logits - row_top[:, None])
        assign = (weights / row_total[:, None]).astype(jnp.bfloat16)
        part_counts = jnp.sum(assign.astype(jnp.float32), axis=0)

        rb = features.shape[1] // nb
        rh = rb // 2

        def part_sums(blk, off):
            col = blk * rb + off
            cblk = col // cw
            if nc == 4:
                t = cblk ^ cme
            else:
                t = (cme - cblk) % nc
            cols = lax.dynamic_slice_in_dim(features, t * cw + col % cw, rh, axis=1)
            return lax.optimization_barrier(
                lax.dot_general(
                    cols, assign, (((0,), (0,)), ((), ())), preferred_element_type=jnp.float32
                )
            )

        def r_step(s, carry):
            acc_a, acc_b, cnt_send, cnt = carry
            ra = lax.ppermute(acc_a.astype(jnp.bfloat16), "blk", fwd)
            rbk = lax.ppermute(acc_b.astype(jnp.bfloat16), "blk", bwd)
            cnt_send = lax.ppermute(cnt_send, "blk", fwd)
            pa = part_sums(ring_blk(p - 1 - s), 0)
            pb = part_sums(ring_blk(p + 1 + s), rh)
            return ra.astype(jnp.float32) + pa, rbk.astype(jnp.float32) + pb, cnt_send, cnt + cnt_send

        acc_a = part_sums(ring_blk(p - 1), 0)
        acc_b = part_sums(ring_blk(p + 1), rh)
        acc_a, acc_b, _, counts = run_steps(
            1, nb, r_step, (acc_a, acc_b, part_counts, part_counts), unroll
        )
        sums = jnp.concatenate([acc_a, acc_b], axis=0)
        return (assign, sums / jnp.maximum(counts, 1.0)[None, :])

    return per_device


def solution(mesh):
    in_specs = (P("blk", None), P("blk", None), P("blk", "cent"), P("cent", None))
    out_specs = (P("blk", "cent"), P("blk", "cent"))
    per_device = make_per_device(mesh.shape["blk"], mesh.shape["cent"])
    return jax.shard_map(
        per_device, mesh=mesh, in_specs=in_specs, out_specs=out_specs, check_vma=False
    )
```

```python
import math

import jax
import jax.numpy as jnp
from jax import lax
from jax.sharding import PartitionSpec as P


def unit_rows(values):
    wide = values.astype(jnp.float32)
    sum_sq = jnp.sum(wide * wide, axis=1, keepdims=True)
    scale = lax.rsqrt(sum_sq + 1e-06)
    return (wide * scale).astype(jnp.bfloat16)


def ring_order(nb):
    if nb % 2:
        return list(range(nb))
    half = nb // 2
    return [2 * i for i in range(half)] + [2 * i + 1 for i in reversed(range(half))]


def run_steps(first, last, step, carry, unroll):
    if unroll:
        for s in range(first, last):
            carry = step(s, carry)
        return carry
    return lax.fori_loop(first, last, step, carry)


def make_per_device(nb, nc):
    ring = ring_order(nb)
    pos_of = [0] * nb
    for i, b in enumerate(ring):
        pos_of[b] = i
    fwd = [(ring[i], ring[(i + 1) % nb]) for i in range(nb)]
    bwd = [(ring[(i + 1) % nb], ring[i]) for i in range(nb)]
    mates = [(c, c ^ 1) for c in range(nc)]
    snake = nb % 2 == 0
    half_nb = nb // 2

    def pos_of_blk(b):
        if not snake:
            return b
        return jnp.where(b % 2 == 0, b // 2, nb - 1 - b // 2)

    def blk_at(i):
        i = i % nb
        if not snake:
            return i
        return jnp.where(i < half_nb, 2 * i, 2 * (nb - 1 - i) + 1)
    unroll = nb <= 8

    def per_device(descriptors, landmarks, whitening, centroids):
        me = lax.axis_index("blk")
        cme = lax.axis_index("cent")
        par = cme % 2
        p = pos_of_blk(me)

        def ring_blk(i):
            return blk_at(i)

        unit_desc = unit_rows(descriptors)
        unit_land = unit_rows(landmarks)
        sharpness = math.sqrt(descriptors.shape[1])
        mw = whitening.shape[0]
        h = mw // 2
        qh = h // 2

        def feat_part(land_rows, w_rows):
            cos = lax.dot_general(
                unit_desc, land_rows, (((1,), (1,)), ((), ())), preferred_element_type=jnp.float32
            )
            kern = jnp.exp(sharpness * cos).astype(jnp.bfloat16)
            return jnp.dot(kern, w_rows, preferred_element_type=jnp.float32)

        la = lax.dynamic_slice_in_dim(unit_land, par * qh, qh, axis=0)
        lb = lax.dynamic_slice_in_dim(unit_land, h + par * qh, qh, axis=0)
        acc = feat_part(unit_land, whitening)

        def mine_first(rows):
            swapped = jnp.concatenate([rows[qh:], rows[:qh]], 0)
            return jnp.where(par == 0, rows, swapped)

        def w_step(s, carry):
            wa, wb, la, lb, acc = carry
            wa = lax.ppermute(wa, "blk", fwd)
            wb = lax.ppermute(wb, "blk", bwd)
            la = lax.ppermute(la, "blk", fwd)
            lb = lax.ppermute(lb, "blk", bwd)
            theirs = lax.ppermute(jnp.concatenate([la, lb], 0), "cent", mates)
            land = jnp.concatenate([la, theirs[:qh], lb, theirs[qh:]], 0)
            wrows = jnp.concatenate([wa, wb], 0)
            acc = lax.optimization_barrier(acc + feat_part(land, wrows))
            return wa, wb, la, lb, acc

        carry = (mine_first(whitening[:h]), mine_first(whitening[h:]), la, lb, acc)
        *_, acc = run_steps(1, nb, w_step, carry, unroll)
        feature_cols = acc.astype(jnp.bfloat16)

        cw = feature_cols.shape[1]
        if nc == 4:
            ypair = [(c, c ^ 2) for c in range(nc)]
            nrow = feature_cols.shape[0]
            nchunk = 4 if nrow % 64 == 0 else 1
            step = nrow // nchunk
            ys, fars = [], []
            for j in range(nchunk):
                y_j = lax.ppermute(feature_cols[j * step:(j + 1) * step], "cent", ypair)
                ys.append(y_j)
                fars.append(lax.ppermute(y_j, "cent", mates))
            from_mate = lax.ppermute(feature_cols, "cent", mates)
            pieces = [feature_cols, from_mate, jnp.concatenate(ys, 0), jnp.concatenate(fars, 0)]
            blocks = [cme ^ t for t in range(nc)]
        else:
            pieces = [feature_cols] + [
                lax.ppermute(feature_cols, "cent", [(c, (c + t) % nc) for c in range(nc)])
                for t in range(1, nc)
            ]
            blocks = [(cme - t) % nc for t in range(nc)]
        logits = None
        for piece, blk in zip(pieces, blocks):
            cpart = lax.dynamic_slice_in_dim(centroids, blk * cw, cw, axis=1)
            part = lax.dot_general(
                piece, cpart, (((1,), (1,)), ((), ())), preferred_element_type=jnp.float32
            )
            logits = part if logits is None else logits + part
        features = jnp.concatenate(pieces, axis=1)
        local_top = jnp.max(logits, axis=1)
        local_sum = jnp.sum(jnp.exp(logits - local_top[:, None]), axis=1)
        stats = jnp.stack([local_top, local_sum], 0)
        peers = [stats] + [
            lax.ppermute(stats, "cent", [(c, (c + k) % nc) for c in range(nc)]) for k in range(1, nc)
        ]
        row_top = peers[0][0]
        for st in peers[1:]:
            row_top = jnp.maximum(row_top, st[0])
        row_total = peers[0][1] * jnp.exp(peers[0][0] - row_top)
        for st in peers[1:]:
            row_total = row_total + st[1] * jnp.exp(st[0] - row_top)
        weights = jnp.exp(logits - row_top[:, None])
        assign = (weights / row_total[:, None]).astype(jnp.bfloat16)
        part_counts = jnp.sum(assign.astype(jnp.float32), axis=0)

        rb = features.shape[1] // nb
        rh = rb // 2

        def part_sums(blk, off):
            col = blk * rb + off
            cblk = col // cw
            if nc == 4:
                t = cblk ^ cme
            else:
                t = (cme - cblk) % nc
            cols = lax.dynamic_slice_in_dim(features, t * cw + col % cw, rh, axis=1)
            return lax.optimization_barrier(
                lax.dot_general(
                    cols, assign, (((0,), (0,)), ((), ())), preferred_element_type=jnp.float32
                )
            )

        def r_step(s, carry):
            acc_a, acc_b, cnt_send, cnt = carry
            ra = lax.ppermute(acc_a.astype(jnp.bfloat16), "blk", fwd)
            rbk = lax.ppermute(acc_b.astype(jnp.bfloat16), "blk", bwd)
            cnt_send = lax.ppermute(cnt_send, "blk", fwd)
            pa = part_sums(ring_blk(p - 1 - s), 0)
            pb = part_sums(ring_blk(p + 1 + s), rh)
            return ra.astype(jnp.float32) + pa, rbk.astype(jnp.float32) + pb, cnt_send, cnt + cnt_send

        acc_a = part_sums(ring_blk(p - 1), 0)
        acc_b = part_sums(ring_blk(p + 1), rh)
        acc_a, acc_b, _, counts = run_steps(
            1, nb, r_step, (acc_a, acc_b, part_counts, part_counts), unroll
        )
        sums = jnp.concatenate([acc_a, acc_b], axis=0)
        return (assign, sums / jnp.maximum(counts, 1.0)[None, :])

    return per_device


def solution(mesh):
    in_specs = (P("blk", None), P("blk", None), P("blk", "cent"), P("cent", None))
    out_specs = (P("blk", "cent"), P("blk", "cent"))
    per_device = make_per_device(mesh.shape["blk"], mesh.shape["cent"])
    return jax.shard_map(
        per_device, mesh=mesh, in_specs=in_specs, out_specs=out_specs, check_vma=False
    )
```

```python
import math

import jax
import jax.numpy as jnp
from jax import lax
from jax.sharding import PartitionSpec as P


def unit_rows(values):
    wide = values.astype(jnp.float32)
    sum_sq = jnp.sum(wide * wide, axis=1, keepdims=True)
    scale = lax.rsqrt(sum_sq + 1e-06)
    return (wide * scale).astype(jnp.bfloat16)


def ring_order(nb):
    if nb % 2:
        return list(range(nb))
    half = nb // 2
    return [2 * i for i in range(half)] + [2 * i + 1 for i in reversed(range(half))]


def run_steps(first, last, step, carry, unroll):
    if unroll:
        for s in range(first, last):
            carry = step(s, carry)
        return carry
    return lax.fori_loop(first, last, step, carry)


def make_per_device(nb, nc):
    ring = ring_order(nb)
    pos_of = [0] * nb
    for i, b in enumerate(ring):
        pos_of[b] = i
    fwd = [(ring[i], ring[(i + 1) % nb]) for i in range(nb)]
    bwd = [(ring[(i + 1) % nb], ring[i]) for i in range(nb)]
    mates = [(c, c ^ 1) for c in range(nc)]
    snake = nb % 2 == 0
    half_nb = nb // 2

    def pos_of_blk(b):
        if not snake:
            return b
        return jnp.where(b % 2 == 0, b // 2, nb - 1 - b // 2)

    def blk_at(i):
        i = i % nb
        if not snake:
            return i
        return jnp.where(i < half_nb, 2 * i, 2 * (nb - 1 - i) + 1)
    unroll = nb <= 8

    def per_device(descriptors, landmarks, whitening, centroids):
        me = lax.axis_index("blk")
        cme = lax.axis_index("cent")
        par = cme % 2
        p = pos_of_blk(me)

        def ring_blk(i):
            return blk_at(i)

        unit_desc = unit_rows(descriptors)
        unit_land = unit_rows(landmarks)
        sharpness = math.sqrt(descriptors.shape[1])
        mw = whitening.shape[0]
        h = mw // 2
        qh = h // 2

        def feat_part(land_rows, w_rows):
            cos = lax.dot_general(
                unit_desc, land_rows, (((1,), (1,)), ((), ())), preferred_element_type=jnp.float32
            )
            kern = jnp.exp(sharpness * cos).astype(jnp.bfloat16)
            return jnp.dot(kern, w_rows, preferred_element_type=jnp.float32)

        la = lax.dynamic_slice_in_dim(unit_land, par * qh, qh, axis=0)
        lb = lax.dynamic_slice_in_dim(unit_land, h + par * qh, qh, axis=0)
        acc = feat_part(unit_land, whitening)

        def mine_first(rows):
            swapped = jnp.concatenate([rows[qh:], rows[:qh]], 0)
            return jnp.where(par == 0, rows, swapped)

        def w_step(s, carry):
            msg_a, msg_b, acc = carry
            msg_a = lax.ppermute(msg_a, "blk", fwd)
            msg_b = lax.ppermute(msg_b, "blk", bwd)
            ta = lax.ppermute(msg_a[h:], "cent", mates)
            tb = lax.ppermute(msg_b[h:], "cent", mates)
            land = jnp.concatenate([msg_a[h:], ta, msg_b[h:], tb], 0)
            wrows = jnp.concatenate([msg_a[:h], msg_b[:h]], 0)
            acc = lax.optimization_barrier(acc + feat_part(land, wrows))
            return msg_a, msg_b, acc

        carry = (
            jnp.concatenate([mine_first(whitening[:h]), la], 0),
            jnp.concatenate([mine_first(whitening[h:]), lb], 0),
            acc,
        )
        *_, acc = run_steps(1, nb, w_step, carry, unroll)
        feature_cols = acc.astype(jnp.bfloat16)

        cw = feature_cols.shape[1]
        if nc == 4:
            ypair = [(c, c ^ 2) for c in range(nc)]
            nrow = feature_cols.shape[0]
            nchunk = 4 if nrow % 64 == 0 else 1
            step = nrow // nchunk
            ys, fars = [], []
            for j in range(nchunk):
                y_j = lax.ppermute(feature_cols[j * step:(j + 1) * step], "cent", ypair)
                ys.append(y_j)
                fars.append(lax.ppermute(y_j, "cent", mates))
            from_mate = lax.ppermute(feature_cols, "cent", mates)
            pieces = [feature_cols, from_mate, jnp.concatenate(ys, 0), jnp.concatenate(fars, 0)]
            blocks = [cme ^ t for t in range(nc)]
        else:
            pieces = [feature_cols] + [
                lax.ppermute(feature_cols, "cent", [(c, (c + t) % nc) for c in range(nc)])
                for t in range(1, nc)
            ]
            blocks = [(cme - t) % nc for t in range(nc)]
        logits = None
        for piece, blk in zip(pieces, blocks):
            cpart = lax.dynamic_slice_in_dim(centroids, blk * cw, cw, axis=1)
            part = lax.dot_general(
                piece, cpart, (((1,), (1,)), ((), ())), preferred_element_type=jnp.float32
            )
            logits = part if logits is None else logits + part
        features = jnp.concatenate(pieces, axis=1)
        local_top = jnp.max(logits, axis=1)
        local_sum = jnp.sum(jnp.exp(logits - local_top[:, None]), axis=1)
        stats = jnp.stack([local_top, local_sum], 0)
        peers = [stats] + [
            lax.ppermute(stats, "cent", [(c, (c + k) % nc) for c in range(nc)]) for k in range(1, nc)
        ]
        row_top = peers[0][0]
        for st in peers[1:]:
            row_top = jnp.maximum(row_top, st[0])
        row_total = peers[0][1] * jnp.exp(peers[0][0] - row_top)
        for st in peers[1:]:
            row_total = row_total + st[1] * jnp.exp(st[0] - row_top)
        weights = jnp.exp(logits - row_top[:, None])
        assign = (weights / row_total[:, None]).astype(jnp.bfloat16)
        part_counts = jnp.sum(assign.astype(jnp.float32), axis=0)

        rb = features.shape[1] // nb
        rh = rb // 2

        def part_sums(blk, off):
            col = blk * rb + off
            cblk = col // cw
            if nc == 4:
                t = cblk ^ cme
            else:
                t = (cme - cblk) % nc
            cols = lax.dynamic_slice_in_dim(features, t * cw + col % cw, rh, axis=1)
            return lax.optimization_barrier(
                lax.dot_general(
                    cols, assign, (((0,), (0,)), ((), ())), preferred_element_type=jnp.float32
                )
            )

        def r_step(s, carry):
            acc_a, acc_b, cnt_send, cnt = carry
            ra = lax.ppermute(acc_a.astype(jnp.bfloat16), "blk", fwd)
            rbk = lax.ppermute(acc_b.astype(jnp.bfloat16), "blk", bwd)
            cnt_send = lax.ppermute(cnt_send, "blk", fwd)
            pa = part_sums(ring_blk(p - 1 - s), 0)
            pb = part_sums(ring_blk(p + 1 + s), rh)
            return ra.astype(jnp.float32) + pa, rbk.astype(jnp.float32) + pb, cnt_send, cnt + cnt_send

        acc_a = part_sums(ring_blk(p - 1), 0)
        acc_b = part_sums(ring_blk(p + 1), rh)
        acc_a, acc_b, _, counts = run_steps(
            1, nb, r_step, (acc_a, acc_b, part_counts, part_counts), unroll
        )
        sums = jnp.concatenate([acc_a, acc_b], axis=0)
        return (assign, sums / jnp.maximum(counts, 1.0)[None, :])

    return per_device


def solution(mesh):
    in_specs = (P("blk", None), P("blk", None), P("blk", "cent"), P("cent", None))
    out_specs = (P("blk", "cent"), P("blk", "cent"))
    per_device = make_per_device(mesh.shape["blk"], mesh.shape["cent"])
    return jax.shard_map(
        per_device, mesh=mesh, in_specs=in_specs, out_specs=out_specs, check_vma=False
    )
```

```python
import math

import jax
import jax.numpy as jnp
from jax import lax
from jax.sharding import PartitionSpec as P


def unit_rows(values):
    wide = values.astype(jnp.float32)
    sum_sq = jnp.sum(wide * wide, axis=1, keepdims=True)
    scale = lax.rsqrt(sum_sq + 1e-06)
    return (wide * scale).astype(jnp.bfloat16)


def ring_order(nb):
    if nb % 2:
        return list(range(nb))
    half = nb // 2
    return [2 * i for i in range(half)] + [2 * i + 1 for i in reversed(range(half))]


def run_steps(first, last, step, carry, unroll):
    if unroll:
        for s in range(first, last):
            carry = step(s, carry)
        return carry
    return lax.fori_loop(first, last, step, carry)


def make_per_device(nb, nc):
    ring = ring_order(nb)
    pos_of = [0] * nb
    for i, b in enumerate(ring):
        pos_of[b] = i
    fwd = [(ring[i], ring[(i + 1) % nb]) for i in range(nb)]
    bwd = [(ring[(i + 1) % nb], ring[i]) for i in range(nb)]
    mates = [(c, c ^ 1) for c in range(nc)]
    snake = nb % 2 == 0
    half_nb = nb // 2

    def pos_of_blk(b):
        if not snake:
            return b
        return jnp.where(b % 2 == 0, b // 2, nb - 1 - b // 2)

    def blk_at(i):
        i = i % nb
        if not snake:
            return i
        return jnp.where(i < half_nb, 2 * i, 2 * (nb - 1 - i) + 1)
    unroll = nb <= 8

    def per_device(descriptors, landmarks, whitening, centroids):
        me = lax.axis_index("blk")
        cme = lax.axis_index("cent")
        par = cme % 2
        p = pos_of_blk(me)

        def ring_blk(i):
            return blk_at(i)

        unit_desc = unit_rows(descriptors)
        unit_land = unit_rows(landmarks)
        sharpness = math.sqrt(descriptors.shape[1])
        mw = whitening.shape[0]
        h = mw // 2
        qh = h // 2

        def feat_part(land_rows, w_rows):
            cos = lax.dot_general(
                unit_desc, land_rows, (((1,), (1,)), ((), ())), preferred_element_type=jnp.float32
            )
            kern = jnp.exp(sharpness * cos).astype(jnp.bfloat16)
            return jnp.dot(kern, w_rows, preferred_element_type=jnp.float32)

        la = lax.dynamic_slice_in_dim(unit_land, par * qh, qh, axis=0)
        lb = lax.dynamic_slice_in_dim(unit_land, h + par * qh, qh, axis=0)
        acc = feat_part(unit_land, whitening)

        def mine_first(rows):
            swapped = jnp.concatenate([rows[qh:], rows[:qh]], 0)
            return jnp.where(par == 0, rows, swapped)

        def w_step(s, carry):
            wa, wb, la, lb, acc = carry
            wa = lax.ppermute(wa, "blk", fwd)
            wb = lax.ppermute(wb, "blk", bwd)
            la = lax.ppermute(la, "blk", fwd)
            lb = lax.ppermute(lb, "blk", bwd)
            ta = lax.ppermute(la, "cent", mates)
            tb = lax.ppermute(lb, "cent", mates)
            land = jnp.concatenate([la, ta, lb, tb], 0)
            wrows = jnp.concatenate([wa, wb], 0)
            acc = lax.optimization_barrier(acc + feat_part(land, wrows))
            return wa, wb, la, lb, acc

        carry = (mine_first(whitening[:h]), mine_first(whitening[h:]), la, lb, acc)
        *_, acc = run_steps(1, nb, w_step, carry, unroll)
        feature_cols = acc.astype(jnp.bfloat16)

        cw = feature_cols.shape[1]
        if nc == 4:
            ypair = [(c, c ^ 2) for c in range(nc)]
            nrow = feature_cols.shape[0]
            nchunk = 4 if nrow % 64 == 0 else 1
            step = nrow // nchunk
            ys, fars = [], []
            for j in range(nchunk):
                y_j = lax.ppermute(feature_cols[j * step:(j + 1) * step], "cent", ypair)
                ys.append(y_j)
                fars.append(lax.ppermute(y_j, "cent", mates))
            from_mate = lax.ppermute(feature_cols, "cent", mates)
            pieces = [feature_cols, from_mate, jnp.concatenate(ys, 0), jnp.concatenate(fars, 0)]
            blocks = [cme ^ t for t in range(nc)]
        else:
            pieces = [feature_cols] + [
                lax.ppermute(feature_cols, "cent", [(c, (c + t) % nc) for c in range(nc)])
                for t in range(1, nc)
            ]
            blocks = [(cme - t) % nc for t in range(nc)]
        logits = None
        for piece, blk in zip(pieces, blocks):
            cpart = lax.dynamic_slice_in_dim(centroids, blk * cw, cw, axis=1)
            part = lax.dot_general(
                piece, cpart, (((1,), (1,)), ((), ())), preferred_element_type=jnp.float32
            )
            logits = part if logits is None else logits + part
        features = jnp.concatenate(pieces, axis=1)
        local_top = jnp.max(logits, axis=1)
        local_sum = jnp.sum(jnp.exp(logits - local_top[:, None]), axis=1)
        stats = jnp.stack([local_top, local_sum], 0)
        peers = [stats] + [
            lax.ppermute(stats, "cent", [(c, (c + k) % nc) for c in range(nc)]) for k in range(1, nc)
        ]
        row_top = peers[0][0]
        for st in peers[1:]:
            row_top = jnp.maximum(row_top, st[0])
        row_total = peers[0][1] * jnp.exp(peers[0][0] - row_top)
        for st in peers[1:]:
            row_total = row_total + st[1] * jnp.exp(st[0] - row_top)
        weights = jnp.exp(logits - row_top[:, None])
        assign = (weights / row_total[:, None]).astype(jnp.bfloat16)
        part_counts = jnp.sum(assign.astype(jnp.float32), axis=0)

        rb = features.shape[1] // nb
        rh = rb // 2

        def part_sums(blk, off):
            col = blk * rb + off
            cblk = col // cw
            if nc == 4:
                t = cblk ^ cme
            else:
                t = (cme - cblk) % nc
            cols = lax.dynamic_slice_in_dim(features, t * cw + col % cw, rh, axis=1)
            return lax.optimization_barrier(
                lax.dot_general(
                    cols, assign, (((0,), (0,)), ((), ())), preferred_element_type=jnp.float32
                )
            )

        def r_step(s, carry):
            acc_a, acc_b, cnt_send, cnt = carry
            ra = lax.ppermute(acc_a.astype(jnp.bfloat16), "blk", fwd)
            rbk = lax.ppermute(acc_b.astype(jnp.bfloat16), "blk", bwd)
            cnt_send = lax.ppermute(cnt_send, "blk", fwd)
            pa = part_sums(ring_blk(p - 1 - s), 0)
            pb = part_sums(ring_blk(p + 1 + s), rh)
            return ra.astype(jnp.float32) + pa, rbk.astype(jnp.float32) + pb, cnt_send, cnt + cnt_send

        acc_a = part_sums(ring_blk(p - 1), 0)
        acc_b = part_sums(ring_blk(p + 1), rh)
        acc_a, acc_b, _, counts = run_steps(
            1, nb, r_step, (acc_a, acc_b, part_counts, part_counts), False
        )
        sums = jnp.concatenate([acc_a, acc_b], axis=0)
        return (assign, sums / jnp.maximum(counts, 1.0)[None, :])

    return per_device


def solution(mesh):
    in_specs = (P("blk", None), P("blk", None), P("blk", "cent"), P("cent", None))
    out_specs = (P("blk", "cent"), P("blk", "cent"))
    per_device = make_per_device(mesh.shape["blk"], mesh.shape["cent"])
    return jax.shard_map(
        per_device, mesh=mesh, in_specs=in_specs, out_specs=out_specs, check_vma=False
    )
```

```python
import math

import jax
import jax.numpy as jnp
from jax import lax
from jax.sharding import PartitionSpec as P


def unit_rows(values):
    wide = values.astype(jnp.float32)
    sum_sq = jnp.sum(wide * wide, axis=1, keepdims=True)
    scale = lax.rsqrt(sum_sq + 1e-06)
    return (wide * scale).astype(jnp.bfloat16)


def ring_order(nb):
    if nb % 2:
        return list(range(nb))
    half = nb // 2
    return [2 * i for i in range(half)] + [2 * i + 1 for i in reversed(range(half))]


def run_steps(first, last, step, carry, unroll):
    if unroll:
        for s in range(first, last):
            carry = step(s, carry)
        return carry
    return lax.fori_loop(first, last, step, carry)


def make_per_device(nb, nc):
    ring = ring_order(nb)
    pos_of = [0] * nb
    for i, b in enumerate(ring):
        pos_of[b] = i
    fwd = [(ring[i], ring[(i + 1) % nb]) for i in range(nb)]
    bwd = [(ring[(i + 1) % nb], ring[i]) for i in range(nb)]
    mates = [(c, c ^ 1) for c in range(nc)]
    snake = nb % 2 == 0
    half_nb = nb // 2

    def pos_of_blk(b):
        if not snake:
            return b
        return jnp.where(b % 2 == 0, b // 2, nb - 1 - b // 2)

    def blk_at(i):
        i = i % nb
        if not snake:
            return i
        return jnp.where(i < half_nb, 2 * i, 2 * (nb - 1 - i) + 1)
    unroll = nb <= 8

    def per_device(descriptors, landmarks, whitening, centroids):
        me = lax.axis_index("blk")
        cme = lax.axis_index("cent")
        par = cme % 2
        p = pos_of_blk(me)

        def ring_blk(i):
            return blk_at(i)

        unit_desc = unit_rows(descriptors)
        unit_land = unit_rows(landmarks)
        sharpness = math.sqrt(descriptors.shape[1])
        mw = whitening.shape[0]
        h = mw // 2
        qh = h // 2

        def feat_part(land_rows, w_rows):
            cos = lax.dot_general(
                unit_desc, land_rows, (((1,), (1,)), ((), ())), preferred_element_type=jnp.float32
            )
            kern = jnp.exp(sharpness * cos).astype(jnp.bfloat16)
            return jnp.dot(kern, w_rows, preferred_element_type=jnp.float32)

        la = lax.dynamic_slice_in_dim(unit_land, par * qh, qh, axis=0)
        lb = lax.dynamic_slice_in_dim(unit_land, h + par * qh, qh, axis=0)
        acc = feat_part(unit_land, whitening)

        def mine_first(rows):
            swapped = jnp.concatenate([rows[qh:], rows[:qh]], 0)
            return jnp.where(par == 0, rows, swapped)

        def w_step(s, carry):
            wa, wb, la, lb, acc = carry
            wa = lax.ppermute(wa, "blk", fwd)
            wb = lax.ppermute(wb, "blk", bwd)
            la = lax.ppermute(la, "blk", fwd)
            lb = lax.ppermute(lb, "blk", bwd)
            ta = lax.ppermute(la, "cent", mates)
            tb = lax.ppermute(lb, "cent", mates)
            land = jnp.concatenate([la, ta, lb, tb], 0)
            wrows = jnp.concatenate([wa, wb], 0)
            acc = lax.optimization_barrier(acc + feat_part(land, wrows))
            return wa, wb, la, lb, acc

        carry = (mine_first(whitening[:h]), mine_first(whitening[h:]), la, lb, acc)
        *_, acc = run_steps(1, nb, w_step, carry, unroll)
        feature_cols = acc.astype(jnp.bfloat16)

        cw = feature_cols.shape[1]
        if nc == 4:
            ypair = [(c, c ^ 2) for c in range(nc)]
            nrow = feature_cols.shape[0]
            nchunk = 4 if nrow % 64 == 0 else 1
            step = nrow // nchunk
            ys, fars = [], []
            for j in range(nchunk):
                y_j = lax.ppermute(feature_cols[j * step:(j + 1) * step], "cent", ypair)
                ys.append(y_j)
                fars.append(lax.ppermute(y_j, "cent", mates))
            from_mate = lax.ppermute(feature_cols, "cent", mates)
            pieces = [feature_cols, from_mate, jnp.concatenate(ys, 0), jnp.concatenate(fars, 0)]
            blocks = [cme ^ t for t in range(nc)]
        else:
            pieces = [feature_cols] + [
                lax.ppermute(feature_cols, "cent", [(c, (c + t) % nc) for c in range(nc)])
                for t in range(1, nc)
            ]
            blocks = [(cme - t) % nc for t in range(nc)]
        logits = None
        for piece, blk in zip(pieces, blocks):
            cpart = lax.dynamic_slice_in_dim(centroids, blk * cw, cw, axis=1)
            part = lax.dot_general(
                piece, cpart, (((1,), (1,)), ((), ())), preferred_element_type=jnp.float32
            )
            logits = part if logits is None else logits + part
        features = jnp.concatenate(pieces, axis=1)
        local_top = jnp.max(logits, axis=1)
        local_sum = jnp.sum(jnp.exp(logits - local_top[:, None]), axis=1)
        stats = jnp.stack([local_top, local_sum], 0)
        peers = [stats] + [
            lax.ppermute(stats, "cent", [(c, (c + k) % nc) for c in range(nc)]) for k in range(1, nc)
        ]
        row_top = peers[0][0]
        for st in peers[1:]:
            row_top = jnp.maximum(row_top, st[0])
        row_total = peers[0][1] * jnp.exp(peers[0][0] - row_top)
        for st in peers[1:]:
            row_total = row_total + st[1] * jnp.exp(st[0] - row_top)
        weights = jnp.exp(logits - row_top[:, None])
        assign = (weights / row_total[:, None]).astype(jnp.bfloat16)
        part_counts = jnp.sum(assign.astype(jnp.float32), axis=0)

        rb = features.shape[1] // nb
        rh = rb // 2

        def part_sums(blk, off):
            col = blk * rb + off
            cblk = col // cw
            if nc == 4:
                t = cblk ^ cme
            else:
                t = (cme - cblk) % nc
            cols = lax.dynamic_slice_in_dim(features, t * cw + col % cw, rh, axis=1)
            return lax.optimization_barrier(
                lax.dot_general(
                    cols, assign, (((0,), (0,)), ((), ())), preferred_element_type=jnp.float32
                )
            )

        def r_step(s, carry):
            acc_a, acc_b, pa, pb, cnt_send, cnt = carry
            ra = lax.ppermute(acc_a.astype(jnp.bfloat16), "blk", fwd)
            rbk = lax.ppermute(acc_b.astype(jnp.bfloat16), "blk", bwd)
            cnt_send = lax.ppermute(cnt_send, "blk", fwd)
            na = part_sums(ring_blk(p - 2 - s), 0)
            nbp = part_sums(ring_blk(p + 2 + s), rh)
            acc_a = ra.astype(jnp.float32) + pa
            acc_b = rbk.astype(jnp.float32) + pb
            return acc_a, acc_b, na, nbp, cnt_send, cnt + cnt_send

        acc_a = part_sums(ring_blk(p - 1), 0)
        acc_b = part_sums(ring_blk(p + 1), rh)
        pa0 = part_sums(ring_blk(p - 2), 0)
        pb0 = part_sums(ring_blk(p + 2), rh)
        acc_a, acc_b, _, _, _, counts = run_steps(
            1, nb, r_step, (acc_a, acc_b, pa0, pb0, part_counts, part_counts), False
        )
        sums = jnp.concatenate([acc_a, acc_b], axis=0)
        return (assign, sums / jnp.maximum(counts, 1.0)[None, :])

    return per_device


def solution(mesh):
    in_specs = (P("blk", None), P("blk", None), P("blk", "cent"), P("cent", None))
    out_specs = (P("blk", "cent"), P("blk", "cent"))
    per_device = make_per_device(mesh.shape["blk"], mesh.shape["cent"])
    return jax.shard_map(
        per_device, mesh=mesh, in_specs=in_specs, out_specs=out_specs, check_vma=False
    )
```

```python
import math

import jax
import jax.numpy as jnp
from jax import lax
from jax.sharding import PartitionSpec as P


def unit_rows(values):
    wide = values.astype(jnp.float32)
    sum_sq = jnp.sum(wide * wide, axis=1, keepdims=True)
    scale = lax.rsqrt(sum_sq + 1e-06)
    return (wide * scale).astype(jnp.bfloat16)


def ring_order(nb):
    if nb % 2:
        return list(range(nb))
    half = nb // 2
    return [2 * i for i in range(half)] + [2 * i + 1 for i in reversed(range(half))]


def run_steps(first, last, step, carry, unroll):
    if unroll:
        for s in range(first, last):
            carry = step(s, carry)
        return carry
    return lax.fori_loop(first, last, step, carry)


def make_per_device(nb, nc):
    ring = ring_order(nb)
    pos_of = [0] * nb
    for i, b in enumerate(ring):
        pos_of[b] = i
    fwd = [(ring[i], ring[(i + 1) % nb]) for i in range(nb)]
    bwd = [(ring[(i + 1) % nb], ring[i]) for i in range(nb)]
    mates = [(c, c ^ 1) for c in range(nc)]
    snake = nb % 2 == 0
    half_nb = nb // 2

    def pos_of_blk(b):
        if not snake:
            return b
        return jnp.where(b % 2 == 0, b // 2, nb - 1 - b // 2)

    def blk_at(i):
        i = i % nb
        if not snake:
            return i
        return jnp.where(i < half_nb, 2 * i, 2 * (nb - 1 - i) + 1)
    unroll = nb <= 8

    def per_device(descriptors, landmarks, whitening, centroids):
        me = lax.axis_index("blk")
        cme = lax.axis_index("cent")
        par = cme % 2
        p = pos_of_blk(me)

        def ring_blk(i):
            return blk_at(i)

        unit_desc = unit_rows(descriptors)
        unit_land = unit_rows(landmarks)
        sharpness = math.sqrt(descriptors.shape[1])
        mw = whitening.shape[0]
        h = mw // 2
        qh = h // 2

        def feat_part(land_rows, w_rows):
            cos = lax.dot_general(
                unit_desc, land_rows, (((1,), (1,)), ((), ())), preferred_element_type=jnp.float32
            )
            kern = jnp.exp(sharpness * cos).astype(jnp.bfloat16)
            return jnp.dot(kern, w_rows, preferred_element_type=jnp.float32)

        la = lax.dynamic_slice_in_dim(unit_land, par * qh, qh, axis=0)
        lb = lax.dynamic_slice_in_dim(unit_land, h + par * qh, qh, axis=0)
        acc = feat_part(unit_land, whitening)

        def mine_first(rows):
            swapped = jnp.concatenate([rows[qh:], rows[:qh]], 0)
            return jnp.where(par == 0, rows, swapped)

        def w_step(s, carry):
            wa, wb, la, lb, acc = carry
            wa = lax.ppermute(wa, "blk", fwd)
            wb = lax.ppermute(wb, "blk", bwd)
            la = lax.ppermute(la, "blk", fwd)
            lb = lax.ppermute(lb, "blk", bwd)
            ta = lax.ppermute(la, "cent", mates)
            tb = lax.ppermute(lb, "cent", mates)
            land = jnp.concatenate([la, ta, lb, tb], 0)
            wrows = jnp.concatenate([wa, wb], 0)
            acc = lax.optimization_barrier(acc + feat_part(land, wrows))
            return wa, wb, la, lb, acc

        carry = (mine_first(whitening[:h]), mine_first(whitening[h:]), la, lb, acc)
        *_, acc = run_steps(1, nb, w_step, carry, unroll)
        feature_cols = acc.astype(jnp.bfloat16)

        cw = feature_cols.shape[1]
        if nc == 4:
            ypair = [(c, c ^ 2) for c in range(nc)]
            nrow = feature_cols.shape[0]
            nchunk = 8 if nrow % 128 == 0 else 1
            step = nrow // nchunk
            ys, fars = [], []
            for j in range(nchunk):
                y_j = lax.ppermute(feature_cols[j * step:(j + 1) * step], "cent", ypair)
                ys.append(y_j)
                fars.append(lax.ppermute(y_j, "cent", mates))
            from_mate = lax.ppermute(feature_cols, "cent", mates)
            pieces = [feature_cols, from_mate, jnp.concatenate(ys, 0), jnp.concatenate(fars, 0)]
            blocks = [cme ^ t for t in range(nc)]
        else:
            pieces = [feature_cols] + [
                lax.ppermute(feature_cols, "cent", [(c, (c + t) % nc) for c in range(nc)])
                for t in range(1, nc)
            ]
            blocks = [(cme - t) % nc for t in range(nc)]
        logits = None
        for piece, blk in zip(pieces, blocks):
            cpart = lax.dynamic_slice_in_dim(centroids, blk * cw, cw, axis=1)
            part = lax.dot_general(
                piece, cpart, (((1,), (1,)), ((), ())), preferred_element_type=jnp.float32
            )
            logits = part if logits is None else logits + part
        features = jnp.concatenate(pieces, axis=1)
        local_top = jnp.max(logits, axis=1)
        local_sum = jnp.sum(jnp.exp(logits - local_top[:, None]), axis=1)
        stats = jnp.stack([local_top, local_sum], 0)
        peers = [stats] + [
            lax.ppermute(stats, "cent", [(c, (c + k) % nc) for c in range(nc)]) for k in range(1, nc)
        ]
        row_top = peers[0][0]
        for st in peers[1:]:
            row_top = jnp.maximum(row_top, st[0])
        row_total = peers[0][1] * jnp.exp(peers[0][0] - row_top)
        for st in peers[1:]:
            row_total = row_total + st[1] * jnp.exp(st[0] - row_top)
        weights = jnp.exp(logits - row_top[:, None])
        assign = (weights / row_total[:, None]).astype(jnp.bfloat16)
        part_counts = jnp.sum(assign.astype(jnp.float32), axis=0)

        rb = features.shape[1] // nb
        rh = rb // 2

        def part_sums(blk, off):
            col = blk * rb + off
            cblk = col // cw
            if nc == 4:
                t = cblk ^ cme
            else:
                t = (cme - cblk) % nc
            cols = lax.dynamic_slice_in_dim(features, t * cw + col % cw, rh, axis=1)
            return lax.optimization_barrier(
                lax.dot_general(
                    cols, assign, (((0,), (0,)), ((), ())), preferred_element_type=jnp.float32
                )
            )

        def r_step(s, carry):
            acc_a, acc_b, cnt_send, cnt = carry
            ra = lax.ppermute(acc_a.astype(jnp.bfloat16), "blk", fwd)
            rbk = lax.ppermute(acc_b.astype(jnp.bfloat16), "blk", bwd)
            cnt_send = lax.ppermute(cnt_send, "blk", fwd)
            pa = part_sums(ring_blk(p - 1 - s), 0)
            pb = part_sums(ring_blk(p + 1 + s), rh)
            return ra.astype(jnp.float32) + pa, rbk.astype(jnp.float32) + pb, cnt_send, cnt + cnt_send

        acc_a = part_sums(ring_blk(p - 1), 0)
        acc_b = part_sums(ring_blk(p + 1), rh)
        acc_a, acc_b, _, counts = run_steps(
            1, nb, r_step, (acc_a, acc_b, part_counts, part_counts), unroll
        )
        sums = jnp.concatenate([acc_a, acc_b], axis=0)
        return (assign, sums / jnp.maximum(counts, 1.0)[None, :])

    return per_device


def solution(mesh):
    in_specs = (P("blk", None), P("blk", None), P("blk", "cent"), P("cent", None))
    out_specs = (P("blk", "cent"), P("blk", "cent"))
    per_device = make_per_device(mesh.shape["blk"], mesh.shape["cent"])
    return jax.shard_map(
        per_device, mesh=mesh, in_specs=in_specs, out_specs=out_specs, check_vma=False
    )
```

```python
import math

import jax
import jax.numpy as jnp
from jax import lax
from jax.sharding import PartitionSpec as P


def unit_rows(values):
    wide = values.astype(jnp.float32)
    sum_sq = jnp.sum(wide * wide, axis=1, keepdims=True)
    scale = lax.rsqrt(sum_sq + 1e-06)
    return (wide * scale).astype(jnp.bfloat16)


def ring_order(nb):
    if nb % 2:
        return list(range(nb))
    half = nb // 2
    return [2 * i for i in range(half)] + [2 * i + 1 for i in reversed(range(half))]


def run_steps(first, last, step, carry, unroll):
    if unroll:
        for s in range(first, last):
            carry = step(s, carry)
        return carry
    return lax.fori_loop(first, last, step, carry)


def make_per_device(nb, nc):
    ring = ring_order(nb)
    pos_of = [0] * nb
    for i, b in enumerate(ring):
        pos_of[b] = i
    fwd = [(ring[i], ring[(i + 1) % nb]) for i in range(nb)]
    bwd = [(ring[(i + 1) % nb], ring[i]) for i in range(nb)]
    mates = [(c, c ^ 1) for c in range(nc)]
    snake = nb % 2 == 0
    half_nb = nb // 2

    def pos_of_blk(b):
        if not snake:
            return b
        return jnp.where(b % 2 == 0, b // 2, nb - 1 - b // 2)

    def blk_at(i):
        i = i % nb
        if not snake:
            return i
        return jnp.where(i < half_nb, 2 * i, 2 * (nb - 1 - i) + 1)
    unroll = nb <= 8

    def per_device(descriptors, landmarks, whitening, centroids):
        me = lax.axis_index("blk")
        cme = lax.axis_index("cent")
        par = cme % 2
        p = pos_of_blk(me)

        def ring_blk(i):
            return blk_at(i)

        unit_desc = unit_rows(descriptors)
        unit_land = unit_rows(landmarks)
        sharpness = math.sqrt(descriptors.shape[1])
        mw = whitening.shape[0]
        h = mw // 2
        qh = h // 2

        def feat_part(land_rows, w_rows):
            cos = lax.dot_general(
                unit_desc, land_rows, (((1,), (1,)), ((), ())), preferred_element_type=jnp.float32
            )
            kern = jnp.exp(sharpness * cos).astype(jnp.bfloat16)
            return jnp.dot(kern, w_rows, preferred_element_type=jnp.float32)

        la = lax.dynamic_slice_in_dim(unit_land, par * qh, qh, axis=0)
        lb = lax.dynamic_slice_in_dim(unit_land, h + par * qh, qh, axis=0)
        acc = feat_part(unit_land, whitening)

        def mine_first(rows):
            swapped = jnp.concatenate([rows[qh:], rows[:qh]], 0)
            return jnp.where(par == 0, rows, swapped)

        def w_step(s, carry):
            wa, wb, la, lb, acc = carry
            wa = lax.ppermute(wa, "blk", fwd)
            wb = lax.ppermute(wb, "blk", bwd)
            la = lax.ppermute(la, "blk", fwd)
            lb = lax.ppermute(lb, "blk", bwd)
            ta = lax.ppermute(la, "cent", mates)
            tb = lax.ppermute(lb, "cent", mates)
            land = jnp.concatenate([la, ta, lb, tb], 0)
            wrows = jnp.concatenate([wa, wb], 0)
            acc = lax.optimization_barrier(acc + feat_part(land, wrows))
            return wa, wb, la, lb, acc

        carry = (mine_first(whitening[:h]), mine_first(whitening[h:]), la, lb, acc)
        *_, acc = run_steps(1, nb, w_step, carry, unroll)
        feature_cols = acc.astype(jnp.bfloat16)

        cw = feature_cols.shape[1]
        if nc == 4:
            ypair = [(c, c ^ 2) for c in range(nc)]
            nrow = feature_cols.shape[0]
            nchunk = 2 if nrow % 32 == 0 else 1
            step = nrow // nchunk
            ys, fars = [], []
            for j in range(nchunk):
                y_j = lax.ppermute(feature_cols[j * step:(j + 1) * step], "cent", ypair)
                ys.append(y_j)
                fars.append(lax.ppermute(y_j, "cent", mates))
            from_mate = lax.ppermute(feature_cols, "cent", mates)
            pieces = [feature_cols, from_mate, jnp.concatenate(ys, 0), jnp.concatenate(fars, 0)]
            blocks = [cme ^ t for t in range(nc)]
        else:
            pieces = [feature_cols] + [
                lax.ppermute(feature_cols, "cent", [(c, (c + t) % nc) for c in range(nc)])
                for t in range(1, nc)
            ]
            blocks = [(cme - t) % nc for t in range(nc)]
        logits = None
        for piece, blk in zip(pieces, blocks):
            cpart = lax.dynamic_slice_in_dim(centroids, blk * cw, cw, axis=1)
            part = lax.dot_general(
                piece, cpart, (((1,), (1,)), ((), ())), preferred_element_type=jnp.float32
            )
            logits = part if logits is None else logits + part
        features = jnp.concatenate(pieces, axis=1)
        local_top = jnp.max(logits, axis=1)
        local_sum = jnp.sum(jnp.exp(logits - local_top[:, None]), axis=1)
        stats = jnp.stack([local_top, local_sum], 0)
        peers = [stats] + [
            lax.ppermute(stats, "cent", [(c, (c + k) % nc) for c in range(nc)]) for k in range(1, nc)
        ]
        row_top = peers[0][0]
        for st in peers[1:]:
            row_top = jnp.maximum(row_top, st[0])
        row_total = peers[0][1] * jnp.exp(peers[0][0] - row_top)
        for st in peers[1:]:
            row_total = row_total + st[1] * jnp.exp(st[0] - row_top)
        weights = jnp.exp(logits - row_top[:, None])
        assign = (weights / row_total[:, None]).astype(jnp.bfloat16)
        part_counts = jnp.sum(assign.astype(jnp.float32), axis=0)

        rb = features.shape[1] // nb
        rh = rb // 2

        def part_sums(blk, off):
            col = blk * rb + off
            cblk = col // cw
            if nc == 4:
                t = cblk ^ cme
            else:
                t = (cme - cblk) % nc
            cols = lax.dynamic_slice_in_dim(features, t * cw + col % cw, rh, axis=1)
            return lax.optimization_barrier(
                lax.dot_general(
                    cols, assign, (((0,), (0,)), ((), ())), preferred_element_type=jnp.float32
                )
            )

        def r_step(s, carry):
            acc_a, acc_b, cnt_send, cnt = carry
            ra = lax.ppermute(acc_a.astype(jnp.bfloat16), "blk", fwd)
            rbk = lax.ppermute(acc_b.astype(jnp.bfloat16), "blk", bwd)
            cnt_send = lax.ppermute(cnt_send, "blk", fwd)
            pa = part_sums(ring_blk(p - 1 - s), 0)
            pb = part_sums(ring_blk(p + 1 + s), rh)
            return ra.astype(jnp.float32) + pa, rbk.astype(jnp.float32) + pb, cnt_send, cnt + cnt_send

        acc_a = part_sums(ring_blk(p - 1), 0)
        acc_b = part_sums(ring_blk(p + 1), rh)
        acc_a, acc_b, _, counts = run_steps(
            1, nb, r_step, (acc_a, acc_b, part_counts, part_counts), unroll
        )
        sums = jnp.concatenate([acc_a, acc_b], axis=0)
        return (assign, sums / jnp.maximum(counts, 1.0)[None, :])

    return per_device


def solution(mesh):
    in_specs = (P("blk", None), P("blk", None), P("blk", "cent"), P("cent", None))
    out_specs = (P("blk", "cent"), P("blk", "cent"))
    per_device = make_per_device(mesh.shape["blk"], mesh.shape["cent"])
    return jax.shard_map(
        per_device, mesh=mesh, in_specs=in_specs, out_specs=out_specs, check_vma=False
    )
```

```python
import math

import jax
import jax.numpy as jnp
from jax import lax
from jax.sharding import PartitionSpec as P


def unit_rows(values):
    wide = values.astype(jnp.float32)
    sum_sq = jnp.sum(wide * wide, axis=1, keepdims=True)
    scale = lax.rsqrt(sum_sq + 1e-06)
    return (wide * scale).astype(jnp.bfloat16)


def ring_order(nb):
    if nb % 2:
        return list(range(nb))
    half = nb // 2
    return [2 * i for i in range(half)] + [2 * i + 1 for i in reversed(range(half))]


def run_steps(first, last, step, carry, unroll):
    if unroll:
        for s in range(first, last):
            carry = step(s, carry)
        return carry
    return lax.fori_loop(first, last, step, carry)


def make_per_device(nb, nc):
    ring = ring_order(nb)
    pos_of = [0] * nb
    for i, b in enumerate(ring):
        pos_of[b] = i
    fwd = [(ring[i], ring[(i + 1) % nb]) for i in range(nb)]
    bwd = [(ring[(i + 1) % nb], ring[i]) for i in range(nb)]
    mates = [(c, c ^ 1) for c in range(nc)]
    snake = nb % 2 == 0
    half_nb = nb // 2

    def pos_of_blk(b):
        if not snake:
            return b
        return jnp.where(b % 2 == 0, b // 2, nb - 1 - b // 2)

    def blk_at(i):
        i = i % nb
        if not snake:
            return i
        return jnp.where(i < half_nb, 2 * i, 2 * (nb - 1 - i) + 1)
    unroll = nb <= 8

    def per_device(descriptors, landmarks, whitening, centroids):
        me = lax.axis_index("blk")
        cme = lax.axis_index("cent")
        par = cme % 2
        p = pos_of_blk(me)

        def ring_blk(i):
            return blk_at(i)

        unit_desc = unit_rows(descriptors)
        unit_land = unit_rows(landmarks)
        sharpness = math.sqrt(descriptors.shape[1])
        mw = whitening.shape[0]
        h = mw // 2
        qh = h // 2

        def feat_part(land_rows, w_rows):
            cos = lax.dot_general(
                unit_desc, land_rows, (((1,), (1,)), ((), ())), preferred_element_type=jnp.float32
            )
            kern = jnp.exp(sharpness * cos).astype(jnp.bfloat16)
            return jnp.dot(kern, w_rows, preferred_element_type=jnp.float32)

        la = lax.dynamic_slice_in_dim(unit_land, par * qh, qh, axis=0)
        lb = lax.dynamic_slice_in_dim(unit_land, h + par * qh, qh, axis=0)
        acc = feat_part(unit_land, whitening)

        def mine_first(rows):
            swapped = jnp.concatenate([rows[qh:], rows[:qh]], 0)
            return jnp.where(par == 0, rows, swapped)

        def w_step(s, carry):
            wa, wb, la, lb, acc = carry
            wa = lax.ppermute(wa, "blk", fwd)
            wb = lax.ppermute(wb, "blk", bwd)
            la = lax.ppermute(la, "blk", fwd)
            lb = lax.ppermute(lb, "blk", bwd)
            ta = lax.ppermute(la, "cent", mates)
            tb = lax.ppermute(lb, "cent", mates)
            land = jnp.concatenate([la, ta, lb, tb], 0)
            wrows = jnp.concatenate([wa, wb], 0)
            acc = lax.optimization_barrier(acc + feat_part(land, wrows))
            return wa, wb, la, lb, acc

        carry = (mine_first(whitening[:h]), mine_first(whitening[h:]), la, lb, acc)
        *_, acc = run_steps(1, nb, w_step, carry, unroll)
        feature_cols = acc.astype(jnp.bfloat16)

        cw = feature_cols.shape[1]
        if nc == 4:
            ypair = [(c, c ^ 2) for c in range(nc)]
            nrow = feature_cols.shape[0]
            nchunk = 4 if nrow % 64 == 0 else 1
            step = nrow // nchunk
            ys, fars = [], []
            for j in range(nchunk):
                y_j = lax.ppermute(feature_cols[j * step:(j + 1) * step], "cent", ypair)
                ys.append(y_j)
                fars.append(lax.ppermute(y_j, "cent", mates))
            from_mate = lax.ppermute(feature_cols, "cent", mates)
            pieces = [feature_cols, from_mate, jnp.concatenate(ys, 0), jnp.concatenate(fars, 0)]
            blocks = [cme ^ t for t in range(nc)]
        else:
            pieces = [feature_cols] + [
                lax.ppermute(feature_cols, "cent", [(c, (c + t) % nc) for c in range(nc)])
                for t in range(1, nc)
            ]
            blocks = [(cme - t) % nc for t in range(nc)]
        logits = None
        for piece, blk in zip(pieces, blocks):
            cpart = lax.dynamic_slice_in_dim(centroids, blk * cw, cw, axis=1)
            part = lax.dot_general(
                piece, cpart, (((1,), (1,)), ((), ())), preferred_element_type=jnp.float32
            )
            logits = part if logits is None else logits + part
        features = jnp.concatenate(pieces, axis=1)
        local_top = jnp.max(logits, axis=1)
        local_sum = jnp.sum(jnp.exp(logits - local_top[:, None]), axis=1)
        stats = jnp.stack([local_top, local_sum], 0)
        peers = [stats] + [
            lax.ppermute(stats, "cent", [(c, (c + k) % nc) for c in range(nc)]) for k in range(1, nc)
        ]
        row_top = peers[0][0]
        for st in peers[1:]:
            row_top = jnp.maximum(row_top, st[0])
        row_total = peers[0][1] * jnp.exp(peers[0][0] - row_top)
        for st in peers[1:]:
            row_total = row_total + st[1] * jnp.exp(st[0] - row_top)
        weights = jnp.exp(logits - row_top[:, None])
        assign = (weights * (1.0 / row_total)[:, None]).astype(jnp.bfloat16)
        part_counts = jnp.sum(assign.astype(jnp.float32), axis=0)

        rb = features.shape[1] // nb
        rh = rb // 2

        def part_sums(blk, off):
            col = blk * rb + off
            cblk = col // cw
            if nc == 4:
                t = cblk ^ cme
            else:
                t = (cme - cblk) % nc
            cols = lax.dynamic_slice_in_dim(features, t * cw + col % cw, rh, axis=1)
            return lax.optimization_barrier(
                lax.dot_general(
                    cols, assign, (((0,), (0,)), ((), ())), preferred_element_type=jnp.float32
                )
            )

        def r_step(s, carry):
            acc_a, acc_b, cnt_send, cnt = carry
            ra = lax.ppermute(acc_a.astype(jnp.bfloat16), "blk", fwd)
            rbk = lax.ppermute(acc_b.astype(jnp.bfloat16), "blk", bwd)
            cnt_send = lax.ppermute(cnt_send, "blk", fwd)
            pa = part_sums(ring_blk(p - 1 - s), 0)
            pb = part_sums(ring_blk(p + 1 + s), rh)
            return ra.astype(jnp.float32) + pa, rbk.astype(jnp.float32) + pb, cnt_send, cnt + cnt_send

        acc_a = part_sums(ring_blk(p - 1), 0)
        acc_b = part_sums(ring_blk(p + 1), rh)
        acc_a, acc_b, _, counts = run_steps(
            1, nb, r_step, (acc_a, acc_b, part_counts, part_counts), unroll
        )
        sums = jnp.concatenate([acc_a, acc_b], axis=0)
        return (assign, sums * (1.0 / jnp.maximum(counts, 1.0))[None, :])

    return per_device


def solution(mesh):
    in_specs = (P("blk", None), P("blk", None), P("blk", "cent"), P("cent", None))
    out_specs = (P("blk", "cent"), P("blk", "cent"))
    per_device = make_per_device(mesh.shape["blk"], mesh.shape["cent"])
    return jax.shard_map(
        per_device, mesh=mesh, in_specs=in_specs, out_specs=out_specs, check_vma=False
    )
```
